256 devices in a mesh: ctx: 32 (over z, x), tp: 8 (over y, core).
Axes of the slice: x: 4, y: 4, z: 8, core: 2. Of those that a mesh axis runs over, the one named last changes fastest.
Arguments:
- tokens: bfloat16 [16384, 3072], P(('ctx', 'tp')), may hold values from -6 to 6
- w_query: bfloat16 [3072, 4096], P(None, 'tp'), may hold values from -0.109375 to 0.109375
- w_key: bfloat16 [3072, 4096], P(None, 'tp'), may hold values from -0.109375 to 0.109375
- w_value: bfloat16 [3072, 4096], P(None, 'tp'), may hold values from -0.109375 to 0.109375
- norm_gain: float32 [4096], P('tp'), may hold values from 0.1 to 1.9
Outputs:
- attended: bfloat16 [16384, 4096], P('ctx', 'tp')
The draws below stay inside these ranges and needn't reach their ends.
All inputs are finite; a program needn't handle non-finite values.
Results may differ from the reference program's by a relative error of at most 0.0062.
Values may be sent and summed in bfloat16 or wider, within the bound.
No kernel may reach another device: no remote copies, remote signals or barrier semaphores. Data moves between devices by JAX's collectives and lax.ppermute only.
A program may use at most 64 MiB of HBM per device.

```python
import jax
import jax.numpy as jnp
from jax import lax

D = 3072
HEADS = 32
HEAD_DIM = 128
BLOCK = 512
TOKENS = 16384


def levels(own_key, shape, split, least, largest):
    level = 1.0
    for axis_at, blocks in split:
        heights = jax.random.uniform(jax.random.fold_in(jax.random.fold_in(own_key, 6), axis_at), (blocks,), jnp.float32, least / len(split), largest / len(split))
        level = level * jnp.repeat(jnp.exp(heights), shape[axis_at] // blocks).reshape((-1,) + (1,) * (len(shape) - 1 - axis_at))
    return level


def bell_draw(own_key, extent, width, bound, pieces=(), held_as=jnp.bfloat16):
    loudness = levels(own_key, extent, pieces, -0.22, 0.18) if pieces else 1.0
    values = jax.random.normal(own_key, extent, jnp.float32) * width * loudness
    return jnp.minimum(jnp.maximum(values, -bound), bound).astype(held_as)


def setup_inputs(seed: int = 0) -> dict:
    splits = jax.random.split(jax.random.key(seed), 6)
    return {
        "tokens": bell_draw(splits[0], (TOKENS, D), 1.0, 6.0, ((0, 256),)),
        "w_query": bell_draw(splits[1], (D, HEADS * HEAD_DIM), D ** -0.5, 0.109375, ((1, 8),)),
        "w_key": bell_draw(splits[2], (D, HEADS * HEAD_DIM), D ** -0.5, 0.109375, ((1, 8),)),
        "w_value": bell_draw(splits[3], (D, HEADS * HEAD_DIM), D ** -0.5, 0.109375, ((1, 8),)),
        "norm_gain": jnp.clip(1.0 + 0.18 * jax.random.normal(splits[4], (HEADS * HEAD_DIM,), jnp.float32), 0.1, 1.9),
    }


EPSILON = 1e-06

def reference(tokens, w_query, w_key, w_value, norm_gain):
    query = jnp.dot(tokens, w_query, preferred_element_type=jnp.float32).astype(jnp.bfloat16)
    key_all = jnp.dot(tokens, w_key, preferred_element_type=jnp.float32).astype(jnp.bfloat16)
    value_all = jnp.dot(tokens, w_value, preferred_element_type=jnp.float32).astype(jnp.bfloat16)
    block_count = TOKENS // BLOCK
    query_blocks = query.reshape(block_count, BLOCK, HEADS, HEAD_DIM)
    key_blocks = key_all.reshape(block_count, BLOCK, HEADS, HEAD_DIM)
    value_blocks = value_all.reshape(block_count, BLOCK, HEADS, HEAD_DIM)
    causal = jnp.arange(BLOCK)[:, None] >= jnp.arange(BLOCK)[None, :]
    highest = lax.Precision.HIGHEST

    def advance(state, blocks):
        query_part, key_part, value_part = blocks
        query_wide = query_part.astype(jnp.float32)
        key_wide = key_part.astype(jnp.float32)
        value_wide = value_part.astype(jnp.float32)
        scores = jnp.einsum('qhd,khd->hqk', query_wide, key_wide, precision=highest)
        scores = jnp.where(causal[None], scores, jnp.float32(0.0))
        scores = lax.optimization_barrier(scores.astype(jnp.bfloat16)).astype(jnp.float32)
        inner = jnp.einsum('hqk,khe->qhe', scores, value_wide, precision=highest)
        carried_part = jnp.einsum('qhd,hde->qhe', query_wide, state, precision=highest)
        new_state = state + jnp.einsum('khd,khe->hde', key_wide, value_wide, precision=highest)
        return (new_state, inner + carried_part)
    start_state = jnp.zeros((HEADS, HEAD_DIM, HEAD_DIM), jnp.float32)
    unused, mixed = lax.scan(advance, start_state, (query_blocks, key_blocks, value_blocks))
    mean_square = lax.optimization_barrier(jnp.mean(mixed * mixed, axis=-1, keepdims=True))
    normed = mixed * lax.rsqrt(mean_square + EPSILON) * norm_gain.reshape(HEADS, HEAD_DIM)
    return normed.reshape(TOKENS, HEADS * HEAD_DIM).astype(jnp.bfloat16)
```

```python
import jax
import jax.numpy as jnp
from jax import lax
from jax.sharding import PartitionSpec as P

HEAD_DIM = 128
BLOCK = 512


EPSILON = 1e-06


def from_behind(value, axis, by):
    size = lax.axis_size(axis)
    pairs = [(i, i + by) for i in range(size) if 0 <= i + by < size]
    return lax.ppermute(value, axis, pairs)


def exclusive_scan(value, axis):
    size = lax.axis_size(axis)
    covered = value
    before = None
    by = 1
    while by < size:
        piece = from_behind(covered, axis, by)
        before = piece if before is None else before + piece
        by *= 2
        if by < size:
            covered = covered + piece
    return before


def body(tokens, w_query, w_key, w_value, norm_gain):
    local_width = w_query.shape[1]
    head_count = local_width // HEAD_DIM
    piece_rows = lax.all_gather(tokens, "tp", axis=0, tiled=True)
    query_part = jnp.dot(piece_rows, w_query, preferred_element_type=jnp.float32).astype(
        jnp.bfloat16
    )
    key_part = jnp.dot(piece_rows, w_key, preferred_element_type=jnp.float32).astype(jnp.bfloat16)
    value_part = jnp.dot(piece_rows, w_value, preferred_element_type=jnp.float32).astype(
        jnp.bfloat16
    )
    projected = jnp.concatenate([query_part, key_part, value_part], axis=1)
    group_len = projected.shape[0]
    block_count = group_len // BLOCK
    shaped = projected.reshape(block_count, BLOCK, 3, head_count, HEAD_DIM)
    query_rows = shaped[:, :, 0]
    key_rows = shaped[:, :, 1]
    value_rows = shaped[:, :, 2]
    block_states = jnp.einsum(
        "bshd,bshe->bhde", key_rows, value_rows, preferred_element_type=jnp.float32
    )
    local_state = jnp.sum(block_states, axis=0)
    prefix_state = exclusive_scan(local_state, "ctx")
    running = jnp.cumsum(block_states, axis=0)
    earlier = jnp.concatenate([jnp.zeros_like(block_states), running[:-1]], axis=0)
    block_start = prefix_state[None] + earlier
    scores = jnp.einsum("bqhd,bkhd->bhqk", query_rows, key_rows, preferred_element_type=jnp.float32)
    causal = jnp.arange(BLOCK)[:, None] >= jnp.arange(BLOCK)[None, :]
    scores = jnp.where(causal[None, None], scores, jnp.float32(0.0)).astype(jnp.bfloat16)
    inner = jnp.einsum("bhqk,bkhe->bqhe", scores, value_rows, preferred_element_type=jnp.float32)
    carried_part = jnp.einsum(
        "bqhd,bhde->bqhe",
        query_rows.astype(jnp.float32),
        block_start,
        precision=lax.Precision.HIGHEST,
    )
    mixed = inner + carried_part
    mean_square = jnp.mean(mixed * mixed, axis=-1, keepdims=True)
    normed = mixed * lax.rsqrt(mean_square + EPSILON) * norm_gain.reshape(head_count, HEAD_DIM)
    return normed.reshape(group_len, local_width).astype(jnp.bfloat16)


def solution(mesh):
    placed = (P(("ctx", "tp"), None), P(None, "tp"), P(None, "tp"), P(None, "tp"), P("tp"))
    return jax.shard_map(
        body, mesh=mesh, in_specs=placed, out_specs=P("ctx", "tp"), check_vma=False
    )
```

```python
import jax
import jax.numpy as jnp
from jax import lax
from jax.sharding import PartitionSpec as P

HEAD_DIM = 128
BLOCK = 512


EPSILON = 1e-06


def from_behind(value, axis, by):
    size = lax.axis_size(axis)
    pairs = [(i, i + by) for i in range(size) if 0 <= i + by < size]
    return lax.ppermute(value, axis, pairs)


def exclusive_scan(value, axis):
    size = lax.axis_size(axis)
    pieces = value.reshape(size, -1, value.shape[-1])
    gathered = lax.all_to_all(pieces, axis, 0, 0, tiled=True)
    running = jnp.cumsum(gathered, axis=0)
    before = jnp.concatenate([jnp.zeros_like(running[:1]), running[:-1]], axis=0)
    returned = lax.all_to_all(before, axis, 0, 0, tiled=True)
    return returned.reshape(value.shape)


def body(tokens, w_query, w_key, w_value, norm_gain):
    local_width = w_query.shape[1]
    head_count = local_width // HEAD_DIM
    piece_rows = lax.all_gather(tokens, "tp", axis=0, tiled=True)
    query_part = jnp.dot(piece_rows, w_query, preferred_element_type=jnp.float32).astype(
        jnp.bfloat16
    )
    key_part = jnp.dot(piece_rows, w_key, preferred_element_type=jnp.float32).astype(jnp.bfloat16)
    value_part = jnp.dot(piece_rows, w_value, preferred_element_type=jnp.float32).astype(
        jnp.bfloat16
    )
    projected = jnp.concatenate([query_part, key_part, value_part], axis=1)
    group_len = projected.shape[0]
    block_count = group_len // BLOCK
    shaped = projected.reshape(block_count, BLOCK, 3, head_count, HEAD_DIM)
    query_rows = shaped[:, :, 0]
    key_rows = shaped[:, :, 1]
    value_rows = shaped[:, :, 2]
    block_states = jnp.einsum(
        "bshd,bshe->bhde", key_rows, value_rows, preferred_element_type=jnp.float32
    )
    local_state = jnp.sum(block_states, axis=0)
    prefix_state = exclusive_scan(local_state, "ctx")
    running = jnp.cumsum(block_states, axis=0)
    earlier = jnp.concatenate([jnp.zeros_like(block_states), running[:-1]], axis=0)
    block_start = prefix_state[None] + earlier
    scores = jnp.einsum("bqhd,bkhd->bhqk", query_rows, key_rows, preferred_element_type=jnp.float32)
    causal = jnp.arange(BLOCK)[:, None] >= jnp.arange(BLOCK)[None, :]
    scores = jnp.where(causal[None, None], scores, jnp.float32(0.0)).astype(jnp.bfloat16)
    inner = jnp.einsum("bhqk,bkhe->bqhe", scores, value_rows, preferred_element_type=jnp.float32)
    carried_part = jnp.einsum(
        "bqhd,bhde->bqhe",
        query_rows.astype(jnp.float32),
        block_start,
        precision=lax.Precision.HIGHEST,
    )
    mixed = inner + carried_part
    mean_square = jnp.mean(mixed * mixed, axis=-1, keepdims=True)
    normed = mixed * lax.rsqrt(mean_square + EPSILON) * norm_gain.reshape(head_count, HEAD_DIM)
    return normed.reshape(group_len, local_width).astype(jnp.bfloat16)


def solution(mesh):
    placed = (P(("ctx", "tp"), None), P(None, "tp"), P(None, "tp"), P(None, "tp"), P("tp"))
    return jax.shard_map(
        body, mesh=mesh, in_specs=placed, out_specs=P("ctx", "tp"), check_vma=False
    )
```

```python
import jax
import jax.numpy as jnp
from jax import lax
from jax.sharding import Mesh, PartitionSpec as P

HEAD_DIM = 128
BLOCK = 512


EPSILON = 1e-06


def from_behind(value, axis, by):
    size = lax.axis_size(axis)
    pairs = [(i, i + by) for i in range(size) if 0 <= i + by < size]
    return lax.ppermute(value, axis, pairs)


def exclusive_scan(value, axis):
    size = lax.axis_size(axis)
    pieces = value.reshape(size, -1, value.shape[-1])
    gathered = lax.all_to_all(pieces, axis, 0, 0, tiled=True)
    running = jnp.cumsum(gathered, axis=0)
    before = jnp.concatenate([jnp.zeros_like(running[:1]), running[:-1]], axis=0)
    returned = lax.all_to_all(before, axis, 0, 0, tiled=True)
    return returned.reshape(value.shape)


def body(tokens, w_query, w_key, w_value, norm_gain):
    local_width = w_query.shape[1]
    head_count = local_width // HEAD_DIM
    near_rows = lax.all_gather(tokens, "y", axis=0, tiled=True)
    both_rows = lax.all_gather(near_rows, "core", axis=0, tiled=False)
    cores, chips = both_rows.shape[0], lax.axis_size("y")
    piece_rows = (
        both_rows.reshape(cores, chips, tokens.shape[0], tokens.shape[1])
        .transpose(1, 0, 2, 3)
        .reshape(cores * chips * tokens.shape[0], tokens.shape[1])
    )
    query_part = jnp.dot(piece_rows, w_query, preferred_element_type=jnp.float32).astype(
        jnp.bfloat16
    )
    key_part = jnp.dot(piece_rows, w_key, preferred_element_type=jnp.float32).astype(jnp.bfloat16)
    value_part = jnp.dot(piece_rows, w_value, preferred_element_type=jnp.float32).astype(
        jnp.bfloat16
    )
    projected = jnp.concatenate([query_part, key_part, value_part], axis=1)
    group_len = projected.shape[0]
    block_count = group_len // BLOCK
    shaped = projected.reshape(block_count, BLOCK, 3, head_count, HEAD_DIM)
    query_rows = shaped[:, :, 0]
    key_rows = shaped[:, :, 1]
    value_rows = shaped[:, :, 2]
    block_states = jnp.einsum(
        "bshd,bshe->bhde", key_rows, value_rows, preferred_element_type=jnp.float32
    )
    local_state = jnp.sum(block_states, axis=0)
    prefix_state = exclusive_scan(local_state, "ctx")
    running = jnp.cumsum(block_states, axis=0)
    earlier = jnp.concatenate([jnp.zeros_like(block_states), running[:-1]], axis=0)
    block_start = prefix_state[None] + earlier
    scores = jnp.einsum("bqhd,bkhd->bhqk", query_rows, key_rows, preferred_element_type=jnp.float32)
    causal = jnp.arange(BLOCK)[:, None] >= jnp.arange(BLOCK)[None, :]
    scores = jnp.where(causal[None, None], scores, jnp.float32(0.0)).astype(jnp.bfloat16)
    inner = jnp.einsum("bhqk,bkhe->bqhe", scores, value_rows, preferred_element_type=jnp.float32)
    carried_part = jnp.einsum(
        "bqhd,bhde->bqhe",
        query_rows.astype(jnp.float32),
        block_start,
        precision=lax.Precision.HIGHEST,
    )
    mixed = inner + carried_part
    mean_square = jnp.mean(mixed * mixed, axis=-1, keepdims=True)
    normed = mixed * lax.rsqrt(mean_square + EPSILON) * norm_gain.reshape(head_count, HEAD_DIM)
    return normed.reshape(group_len, local_width).astype(jnp.bfloat16)


def chip_split(mesh):
    first = mesh.devices[0]
    cores = len({getattr(device, "core_on_chip", 0) for device in first})
    return mesh.devices.reshape(mesh.devices.shape[0], -1, cores)


def solution(mesh):
    fine = Mesh(chip_split(mesh), ("ctx", "y", "core"))
    heads = ("y", "core")
    placed = (P(("ctx",) + heads, None), P(None, heads), P(None, heads), P(None, heads), P(heads))
    return jax.shard_map(
        body, mesh=fine, in_specs=placed, out_specs=P("ctx", heads), check_vma=False
    )
```

```python
import jax
import jax.numpy as jnp
from jax import lax
from jax.sharding import Mesh, PartitionSpec as P

HEAD_DIM = 128
BLOCK = 512


EPSILON = 1e-06


def from_behind(value, axis, by):
    size = lax.axis_size(axis)
    pairs = [(i, i + by) for i in range(size) if 0 <= i + by < size]
    return lax.ppermute(value, axis, pairs)


def exclusive_scan(value, axis):
    size = lax.axis_size(axis)
    pieces = value.reshape(size, -1, value.shape[-1])
    gathered = lax.all_to_all(pieces, axis, 0, 0, tiled=True)
    running = jnp.cumsum(gathered, axis=0)
    before = jnp.concatenate([jnp.zeros_like(running[:1]), running[:-1]], axis=0)
    returned = lax.all_to_all(before, axis, 0, 0, tiled=True)
    return returned.reshape(value.shape)


def spread(value, axis):
    size = lax.axis_size(axis)
    copies = jnp.broadcast_to(value[None], (size,) + value.shape)
    return lax.all_to_all(copies, axis, 0, 0, tiled=True)


def gather_rows(tokens):
    near = spread(tokens, "y")
    both = spread(near, "core")
    return both.transpose(1, 0, 2, 3).reshape(-1, tokens.shape[1])


def body(tokens, w_query, w_key, w_value, norm_gain):
    local_width = w_query.shape[1]
    head_count = local_width // HEAD_DIM
    piece_rows = gather_rows(tokens)
    query_part = jnp.dot(piece_rows, w_query, preferred_element_type=jnp.float32).astype(
        jnp.bfloat16
    )
    key_part = jnp.dot(piece_rows, w_key, preferred_element_type=jnp.float32).astype(jnp.bfloat16)
    value_part = jnp.dot(piece_rows, w_value, preferred_element_type=jnp.float32).astype(
        jnp.bfloat16
    )
    projected = jnp.concatenate([query_part, key_part, value_part], axis=1)
    group_len = projected.shape[0]
    block_count = group_len // BLOCK
    shaped = projected.reshape(block_count, BLOCK, 3, head_count, HEAD_DIM)
    query_rows = shaped[:, :, 0]
    key_rows = shaped[:, :, 1]
    value_rows = shaped[:, :, 2]
    block_states = jnp.einsum(
        "bshd,bshe->bhde", key_rows, value_rows, preferred_element_type=jnp.float32
    )
    local_state = jnp.sum(block_states, axis=0)
    prefix_state = exclusive_scan(local_state, "ctx")
    running = jnp.cumsum(block_states, axis=0)
    earlier = jnp.concatenate([jnp.zeros_like(block_states), running[:-1]], axis=0)
    block_start = prefix_state[None] + earlier
    scores = jnp.einsum("bqhd,bkhd->bhqk", query_rows, key_rows, preferred_element_type=jnp.float32)
    causal = jnp.arange(BLOCK)[:, None] >= jnp.arange(BLOCK)[None, :]
    scores = jnp.where(causal[None, None], scores, jnp.float32(0.0)).astype(jnp.bfloat16)
    inner = jnp.einsum("bhqk,bkhe->bqhe", scores, value_rows, preferred_element_type=jnp.float32)
    carried_part = jnp.einsum(
        "bqhd,bhde->bqhe",
        query_rows.astype(jnp.float32),
        block_start,
        precision=lax.Precision.HIGHEST,
    )
    mixed = inner + carried_part
    mean_square = jnp.mean(mixed * mixed, axis=-1, keepdims=True)
    normed = mixed * lax.rsqrt(mean_square + EPSILON) * norm_gain.reshape(head_count, HEAD_DIM)
    return normed.reshape(group_len, local_width).astype(jnp.bfloat16)


def chip_split(mesh):
    first = mesh.devices[0]
    cores = len({getattr(device, "core_on_chip", 0) for device in first})
    return mesh.devices.reshape(mesh.devices.shape[0], -1, cores)


def solution(mesh):
    fine = Mesh(chip_split(mesh), ("ctx", "y", "core"))
    heads = ("y", "core")
    placed = (P(("ctx",) + heads, None), P(None, heads), P(None, heads), P(None, heads), P(heads))
    return jax.shard_map(
        body, mesh=fine, in_specs=placed, out_specs=P("ctx", heads), check_vma=False
    )
```

```python
import jax
import jax.numpy as jnp
from jax import lax
from jax.sharding import Mesh, PartitionSpec as P

HEAD_DIM = 128
BLOCK = 512


EPSILON = 1e-06


def from_behind(value, axis, by):
    size = lax.axis_size(axis)
    pairs = [(i, i + by) for i in range(size) if 0 <= i + by < size]
    return lax.ppermute(value, axis, pairs)


def exclusive_scan(value, axis):
    size = lax.axis_size(axis)
    pieces = value.reshape(size, -1, value.shape[-1])
    gathered = lax.all_to_all(pieces, axis, 0, 0, tiled=True)
    earlier = jnp.arange(size)[:, None] > jnp.arange(size)[None, :]
    before = jnp.einsum(
        "jk,kre->jre",
        earlier.astype(gathered.dtype),
        gathered,
        precision=lax.Precision.HIGHEST,
    )
    returned = lax.all_to_all(before, axis, 0, 0, tiled=True)
    return returned.reshape(value.shape)


def spread(value, axis):
    size = lax.axis_size(axis)
    copies = jnp.broadcast_to(value[None], (size,) + value.shape)
    return lax.all_to_all(copies, axis, 0, 0, tiled=True)


def gather_rows(tokens):
    near = spread(tokens, "y")
    both = spread(near, "core")
    return both.transpose(1, 0, 2, 3).reshape(-1, tokens.shape[1])


def body(tokens, w_query, w_key, w_value, norm_gain):
    local_width = w_query.shape[1]
    head_count = local_width // HEAD_DIM
    piece_rows = gather_rows(tokens)
    query_part = jnp.dot(piece_rows, w_query, preferred_element_type=jnp.float32).astype(
        jnp.bfloat16
    )
    key_part = jnp.dot(piece_rows, w_key, preferred_element_type=jnp.float32).astype(jnp.bfloat16)
    value_part = jnp.dot(piece_rows, w_value, preferred_element_type=jnp.float32).astype(
        jnp.bfloat16
    )
    projected = jnp.concatenate([query_part, key_part, value_part], axis=1)
    group_len = projected.shape[0]
    block_count = group_len // BLOCK
    shaped = projected.reshape(block_count, BLOCK, 3, head_count, HEAD_DIM)
    query_rows = shaped[:, :, 0]
    key_rows = shaped[:, :, 1]
    value_rows = shaped[:, :, 2]
    block_states = jnp.einsum(
        "bshd,bshe->bhde", key_rows, value_rows, preferred_element_type=jnp.float32
    )
    local_state = jnp.sum(block_states, axis=0)
    prefix_state = exclusive_scan(local_state, "ctx")
    running = jnp.cumsum(block_states, axis=0)
    earlier = jnp.concatenate([jnp.zeros_like(block_states), running[:-1]], axis=0)
    block_start = prefix_state[None] + earlier
    scores = jnp.einsum("bqhd,bkhd->bhqk", query_rows, key_rows, preferred_element_type=jnp.float32)
    causal = jnp.arange(BLOCK)[:, None] >= jnp.arange(BLOCK)[None, :]
    scores = jnp.where(causal[None, None], scores, jnp.float32(0.0)).astype(jnp.bfloat16)
    inner = jnp.einsum("bhqk,bkhe->bqhe", scores, value_rows, preferred_element_type=jnp.float32)
    inner = lax.optimization_barrier(inner)
    start_high = block_start.astype(jnp.bfloat16)
    start_low = (block_start - start_high.astype(jnp.float32)).astype(jnp.bfloat16)
    carried_part = jnp.einsum(
        "bqhd,bhde->bqhe", query_rows, start_high, preferred_element_type=jnp.float32
    ) + jnp.einsum("bqhd,bhde->bqhe", query_rows, start_low, preferred_element_type=jnp.float32)
    mixed = inner + carried_part
    mean_square = jnp.mean(mixed * mixed, axis=-1, keepdims=True)
    normed = mixed * lax.rsqrt(mean_square + EPSILON) * norm_gain.reshape(head_count, HEAD_DIM)
    return normed.reshape(group_len, local_width).astype(jnp.bfloat16)


def chip_split(mesh):
    first = mesh.devices[0]
    cores = len({getattr(device, "core_on_chip", 0) for device in first})
    return mesh.devices.reshape(mesh.devices.shape[0], -1, cores)


def solution(mesh):
    fine = Mesh(chip_split(mesh), ("ctx", "y", "core"))
    heads = ("y", "core")
    placed = (P(("ctx",) + heads, None), P(None, heads), P(None, heads), P(None, heads), P(heads))
    return jax.shard_map(
        body, mesh=fine, in_specs=placed, out_specs=P("ctx", heads), check_vma=False
    )
```

```python
import jax
import jax.numpy as jnp
from jax import lax
from jax.sharding import Mesh, PartitionSpec as P

HEAD_DIM = 128
BLOCK = 512


EPSILON = 1e-06


def from_behind(value, axis, by):
    size = lax.axis_size(axis)
    pairs = [(i, i + by) for i in range(size) if 0 <= i + by < size]
    return lax.ppermute(value, axis, pairs)


def exclusive_scan(value, axis):
    size = lax.axis_size(axis)
    pieces = value.reshape(size, -1, value.shape[-1])
    gathered = lax.all_to_all(pieces, axis, 0, 0, tiled=True)
    earlier = jnp.arange(size)[:, None] > jnp.arange(size)[None, :]
    before = jnp.dot(
        earlier.astype(gathered.dtype),
        gathered.reshape(size, -1),
        precision=lax.Precision.HIGHEST,
    ).reshape(pieces.shape)
    returned = lax.all_to_all(before, axis, 0, 0, tiled=True)
    return returned.reshape(value.shape)


def spread(value, axis):
    size = lax.axis_size(axis)
    copies = jnp.broadcast_to(value[None], (size,) + value.shape)
    return lax.all_to_all(copies, axis, 0, 0, tiled=True)


def gather_rows(tokens):
    near = spread(tokens, "y")
    both = spread(near, "core")
    return both.transpose(1, 0, 2, 3).reshape(-1, tokens.shape[1])


def body(tokens, w_query, w_key, w_value, norm_gain):
    local_width = w_query.shape[1]
    head_count = local_width // HEAD_DIM
    piece_rows = gather_rows(tokens)
    query_part = jnp.dot(piece_rows, w_query, preferred_element_type=jnp.float32).astype(
        jnp.bfloat16
    )
    key_part = jnp.dot(piece_rows, w_key, preferred_element_type=jnp.float32).astype(jnp.bfloat16)
    value_part = jnp.dot(piece_rows, w_value, preferred_element_type=jnp.float32).astype(
        jnp.bfloat16
    )
    projected = jnp.concatenate([query_part, key_part, value_part], axis=1)
    group_len = projected.shape[0]
    block_count = group_len // BLOCK
    shaped = projected.reshape(block_count, BLOCK, 3, head_count, HEAD_DIM)
    query_rows = shaped[:, :, 0]
    key_rows = shaped[:, :, 1]
    value_rows = shaped[:, :, 2]
    block_states = jnp.einsum(
        "bshd,bshe->bhde", key_rows, value_rows, preferred_element_type=jnp.float32
    )
    local_state = jnp.sum(block_states, axis=0)
    prefix_state = exclusive_scan(local_state, "ctx")
    running = jnp.cumsum(block_states, axis=0)
    earlier = jnp.concatenate([jnp.zeros_like(block_states), running[:-1]], axis=0)
    block_start = prefix_state[None] + earlier
    scores = jnp.einsum("bqhd,bkhd->bhqk", query_rows, key_rows, preferred_element_type=jnp.float32)
    causal = jnp.arange(BLOCK)[:, None] >= jnp.arange(BLOCK)[None, :]
    scores = jnp.where(causal[None, None], scores, jnp.float32(0.0)).astype(jnp.bfloat16)
    inner = jnp.einsum("bhqk,bkhe->bqhe", scores, value_rows, preferred_element_type=jnp.float32)
    inner = lax.optimization_barrier(inner)
    start_high = lax.optimization_barrier(block_start.astype(jnp.bfloat16))
    start_low = (block_start - start_high.astype(jnp.float32)).astype(jnp.bfloat16)
    carried_part = jnp.einsum(
        "bqhd,bhde->bqhe", query_rows, start_high, preferred_element_type=jnp.float32
    ) + jnp.einsum("bqhd,bhde->bqhe", query_rows, start_low, preferred_element_type=jnp.float32)
    mixed = inner + carried_part
    mean_square = jnp.mean(mixed * mixed, axis=-1, keepdims=True)
    normed = mixed * lax.rsqrt(mean_square + EPSILON) * norm_gain.reshape(head_count, HEAD_DIM)
    return normed.reshape(group_len, local_width).astype(jnp.bfloat16)


def chip_split(mesh):
    first = mesh.devices[0]
    cores = len({getattr(device, "core_on_chip", 0) for device in first})
    return mesh.devices.reshape(mesh.devices.shape[0], -1, cores)


def solution(mesh):
    fine = Mesh(chip_split(mesh), ("ctx", "y", "core"))
    heads = ("y", "core")
    placed = (P(("ctx",) + heads, None), P(None, heads), P(None, heads), P(None, heads), P(heads))
    return jax.shard_map(
        body, mesh=fine, in_specs=placed, out_specs=P("ctx", heads), check_vma=False
    )
```

```python
import jax
import jax.numpy as jnp
from jax import lax
from jax.sharding import Mesh, PartitionSpec as P

HEAD_DIM = 128
BLOCK = 512


EPSILON = 1e-06


def from_behind(value, axis, by):
    size = lax.axis_size(axis)
    pairs = [(i, i + by) for i in range(size) if 0 <= i + by < size]
    return lax.ppermute(value, axis, pairs)


def exclusive_scan(value, axis):
    size = lax.axis_size(axis)
    pieces = value.reshape(size, -1, value.shape[-1]).astype(jnp.bfloat16)
    gathered = lax.all_to_all(pieces, axis, 0, 0, tiled=True)
    earlier = jnp.arange(size)[:, None] > jnp.arange(size)[None, :]
    before = jnp.dot(
        earlier.astype(gathered.dtype),
        gathered.reshape(size, -1),
        preferred_element_type=jnp.float32,
    ).astype(jnp.bfloat16)
    returned = lax.all_to_all(before.reshape(pieces.shape), axis, 0, 0, tiled=True)
    return returned.reshape(value.shape)


def spread(value, axis):
    size = lax.axis_size(axis)
    copies = jnp.broadcast_to(value[None], (size,) + value.shape)
    return lax.all_to_all(copies, axis, 0, 0, tiled=True)


def gather_rows(tokens):
    near = spread(tokens, "y")
    both = spread(near, "core")
    return both.transpose(1, 0, 2, 3).reshape(-1, tokens.shape[1])


def body(tokens, w_query, w_key, w_value, norm_gain):
    local_width = w_query.shape[1]
    head_count = local_width // HEAD_DIM
    piece_rows = gather_rows(tokens)
    query_part = jnp.dot(piece_rows, w_query, preferred_element_type=jnp.float32).astype(
        jnp.bfloat16
    )
    key_part = jnp.dot(piece_rows, w_key, preferred_element_type=jnp.float32).astype(jnp.bfloat16)
    value_part = jnp.dot(piece_rows, w_value, preferred_element_type=jnp.float32).astype(
        jnp.bfloat16
    )
    projected = jnp.concatenate([query_part, key_part, value_part], axis=1)
    group_len = projected.shape[0]
    block_count = group_len // BLOCK
    shaped = projected.reshape(block_count, BLOCK, 3, head_count, HEAD_DIM)
    query_rows = shaped[:, :, 0]
    key_rows = shaped[:, :, 1]
    value_rows = shaped[:, :, 2]
    block_states = jnp.einsum(
        "bshd,bshe->bhde", key_rows, value_rows, preferred_element_type=jnp.float32
    )
    local_state = jnp.sum(block_states, axis=0)
    prefix_state = exclusive_scan(local_state, "ctx")
    running = jnp.cumsum(block_states, axis=0)
    earlier = jnp.concatenate([jnp.zeros_like(block_states), running[:-1]], axis=0)
    block_start = (prefix_state.astype(jnp.float32)[None] + earlier).astype(jnp.bfloat16)
    scores = jnp.einsum("bqhd,bkhd->bhqk", query_rows, key_rows, preferred_element_type=jnp.float32)
    causal = jnp.arange(BLOCK)[:, None] >= jnp.arange(BLOCK)[None, :]
    scores = jnp.where(causal[None, None], scores, jnp.float32(0.0)).astype(jnp.bfloat16)
    inner = jnp.einsum("bhqk,bkhe->bqhe", scores, value_rows, preferred_element_type=jnp.float32)
    inner = lax.optimization_barrier(inner)
    carried_part = jnp.einsum(
        "bqhd,bhde->bqhe", query_rows, block_start, preferred_element_type=jnp.float32
    )
    mixed = inner + carried_part
    mean_square = jnp.mean(mixed * mixed, axis=-1, keepdims=True)
    normed = mixed * lax.rsqrt(mean_square + EPSILON) * norm_gain.reshape(head_count, HEAD_DIM)
    return normed.reshape(group_len, local_width).astype(jnp.bfloat16)


def chip_split(mesh):
    first = mesh.devices[0]
    cores = len({getattr(device, "core_on_chip", 0) for device in first})
    return mesh.devices.reshape(mesh.devices.shape[0], -1, cores)


def solution(mesh):
    fine = Mesh(chip_split(mesh), ("ctx", "y", "core"))
    heads = ("y", "core")
    placed = (P(("ctx",) + heads, None), P(None, heads), P(None, heads), P(None, heads), P(heads))
    return jax.shard_map(
        body, mesh=fine, in_specs=placed, out_specs=P("ctx", heads), check_vma=False
    )
```

```python
import jax
import jax.numpy as jnp
from jax import lax
from jax.sharding import Mesh, PartitionSpec as P

HEAD_DIM = 128
BLOCK = 512


EPSILON = 1e-06


def from_behind(value, axis, by):
    size = lax.axis_size(axis)
    pairs = [(i, i + by) for i in range(size) if 0 <= i + by < size]
    return lax.ppermute(value, axis, pairs)


def exclusive_scan(value, axis):
    size = lax.axis_size(axis)
    pieces = value.reshape(size, -1, value.shape[-1]).astype(jnp.bfloat16)
    gathered = lax.all_to_all(pieces, axis, 0, 0, tiled=True)
    earlier = jnp.arange(size)[:, None] > jnp.arange(size)[None, :]
    before = jnp.dot(
        earlier.astype(gathered.dtype),
        gathered.reshape(size, -1),
        preferred_element_type=jnp.float32,
    ).astype(jnp.bfloat16)
    returned = lax.all_to_all(before.reshape(pieces.shape), axis, 0, 0, tiled=True)
    return returned.reshape(value.shape)


def spread(value, axis):
    size = lax.axis_size(axis)
    copies = jnp.broadcast_to(value[None], (size,) + value.shape)
    return lax.all_to_all(copies, axis, 0, 0, tiled=True)


def gather_rows(tokens):
    near = spread(tokens, "y")
    both = spread(near, "core")
    return both.transpose(1, 0, 2, 3).reshape(-1, tokens.shape[1])


def body(tokens, w_query, w_key, w_value, norm_gain):
    local_width = w_query.shape[1]
    head_count = local_width // HEAD_DIM
    piece_rows = gather_rows(tokens)
    group_len = piece_rows.shape[0]
    block_count = group_len // BLOCK

    def project(weight):
        part = jnp.dot(piece_rows_now, weight, preferred_element_type=jnp.float32)
        return part.astype(jnp.bfloat16).reshape(block_count, BLOCK, head_count, HEAD_DIM)

    piece_rows_now = piece_rows
    key_rows = project(w_key)
    value_rows = project(w_value)
    block_states = jnp.einsum(
        "bshd,bshe->bhde", key_rows, value_rows, preferred_element_type=jnp.float32
    )
    local_state = jnp.sum(block_states, axis=0)
    piece_rows_now, local_state = lax.optimization_barrier((piece_rows, local_state))
    query_rows = project(w_query)
    prefix_state = exclusive_scan(local_state, "ctx")
    running = jnp.cumsum(block_states, axis=0)
    earlier = jnp.concatenate([jnp.zeros_like(block_states), running[:-1]], axis=0)
    block_start = (prefix_state.astype(jnp.float32)[None] + earlier).astype(jnp.bfloat16)
    scores = jnp.einsum("bqhd,bkhd->bhqk", query_rows, key_rows, preferred_element_type=jnp.float32)
    causal = jnp.arange(BLOCK)[:, None] >= jnp.arange(BLOCK)[None, :]
    scores = jnp.where(causal[None, None], scores, jnp.float32(0.0)).astype(jnp.bfloat16)
    inner = jnp.einsum("bhqk,bkhe->bqhe", scores, value_rows, preferred_element_type=jnp.float32)
    inner = lax.optimization_barrier(inner)
    carried_part = jnp.einsum(
        "bqhd,bhde->bqhe", query_rows, block_start, preferred_element_type=jnp.float32
    )
    mixed = inner + carried_part
    mean_square = jnp.mean(mixed * mixed, axis=-1, keepdims=True)
    normed = mixed * lax.rsqrt(mean_square + EPSILON) * norm_gain.reshape(head_count, HEAD_DIM)
    return normed.reshape(group_len, local_width).astype(jnp.bfloat16)


def chip_split(mesh):
    first = mesh.devices[0]
    cores = len({getattr(device, "core_on_chip", 0) for device in first})
    return mesh.devices.reshape(mesh.devices.shape[0], -1, cores)


def solution(mesh):
    fine = Mesh(chip_split(mesh), ("ctx", "y", "core"))
    heads = ("y", "core")
    placed = (P(("ctx",) + heads, None), P(None, heads), P(None, heads), P(None, heads), P(heads))
    return jax.shard_map(
        body, mesh=fine, in_specs=placed, out_specs=P("ctx", heads), check_vma=False
    )
```

```python
import jax
import jax.numpy as jnp
from jax import lax
from jax.sharding import Mesh, PartitionSpec as P

HEAD_DIM = 128
BLOCK = 512


EPSILON = 1e-06


def from_behind(value, axis, by):
    size = lax.axis_size(axis)
    pairs = [(i, i + by) for i in range(size) if 0 <= i + by < size]
    return lax.ppermute(value, axis, pairs)


def exclusive_scan(value, axis):
    size = lax.axis_size(axis)
    pieces = value.reshape(size, -1, value.shape[-1]).astype(jnp.bfloat16)
    gathered = lax.all_to_all(pieces, axis, 0, 0, tiled=True)
    earlier = jnp.arange(size)[:, None] > jnp.arange(size)[None, :]
    before = jnp.dot(
        earlier.astype(gathered.dtype),
        gathered.reshape(size, -1),
        preferred_element_type=jnp.float32,
    ).astype(jnp.bfloat16)
    returned = lax.all_to_all(before.reshape(pieces.shape), axis, 0, 0, tiled=True)
    return returned.reshape(value.shape)


def gather_rows(tokens):
    chips = lax.axis_size("y")
    chip = lax.axis_index("y")
    ahead = [tokens] + [
        lax.ppermute(tokens, "y", [(i, (i - by) % chips) for i in range(chips)])
        for by in range(1, chips)
    ]
    twice = jnp.stack(ahead + ahead)
    near = lax.dynamic_slice_in_dim(twice, (chips - chip) % chips, chips, axis=0)
    other = lax.ppermute(near, "core", [(0, 1), (1, 0)])
    trio = jnp.stack([near, other, near], axis=1)
    both = lax.dynamic_slice_in_dim(trio, lax.axis_index("core"), 2, axis=1)
    return both.reshape(-1, tokens.shape[1])


def body(tokens, w_query, w_key, w_value, norm_gain):
    local_width = w_query.shape[1]
    head_count = local_width // HEAD_DIM
    piece_rows = gather_rows(tokens)
    query_part = jnp.dot(piece_rows, w_query, preferred_element_type=jnp.float32).astype(
        jnp.bfloat16
    )
    key_part = jnp.dot(piece_rows, w_key, preferred_element_type=jnp.float32).astype(jnp.bfloat16)
    value_part = jnp.dot(piece_rows, w_value, preferred_element_type=jnp.float32).astype(
        jnp.bfloat16
    )
    projected = jnp.concatenate([query_part, key_part, value_part], axis=1)
    group_len = projected.shape[0]
    block_count = group_len // BLOCK
    shaped = projected.reshape(block_count, BLOCK, 3, head_count, HEAD_DIM)
    query_rows = shaped[:, :, 0]
    key_rows = shaped[:, :, 1]
    value_rows = shaped[:, :, 2]
    block_states = jnp.einsum(
        "bshd,bshe->bhde", key_rows, value_rows, preferred_element_type=jnp.float32
    )
    local_state = jnp.sum(block_states, axis=0)
    prefix_state = exclusive_scan(local_state, "ctx")
    running = jnp.cumsum(block_states, axis=0)
    earlier = jnp.concatenate([jnp.zeros_like(block_states), running[:-1]], axis=0)
    block_start = (prefix_state.astype(jnp.float32)[None] + earlier).astype(jnp.bfloat16)
    scores = jnp.einsum("bqhd,bkhd->bhqk", query_rows, key_rows, preferred_element_type=jnp.float32)
    causal = jnp.arange(BLOCK)[:, None] >= jnp.arange(BLOCK)[None, :]
    scores = jnp.where(causal[None, None], scores, jnp.float32(0.0)).astype(jnp.bfloat16)
    inner = jnp.einsum("bhqk,bkhe->bqhe", scores, value_rows, preferred_element_type=jnp.float32)
    inner = lax.optimization_barrier(inner)
    carried_part = jnp.einsum(
        "bqhd,bhde->bqhe", query_rows, block_start, preferred_element_type=jnp.float32
    )
    mixed = inner + carried_part
    mean_square = jnp.mean(mixed * mixed, axis=-1, keepdims=True)
    normed = mixed * lax.rsqrt(mean_square + EPSILON) * norm_gain.reshape(head_count, HEAD_DIM)
    return normed.reshape(group_len, local_width).astype(jnp.bfloat16)


def chip_split(mesh):
    first = mesh.devices[0]
    cores = len({getattr(device, "core_on_chip", 0) for device in first})
    return mesh.devices.reshape(mesh.devices.shape[0], -1, cores)


def solution(mesh):
    fine = Mesh(chip_split(mesh), ("ctx", "y", "core"))
    heads = ("y", "core")
    placed = (P(("ctx",) + heads, None), P(None, heads), P(None, heads), P(None, heads), P(heads))
    return jax.shard_map(
        body, mesh=fine, in_specs=placed, out_specs=P("ctx", heads), check_vma=False
    )
```

```python
import jax
import jax.numpy as jnp
from jax import lax
from jax.sharding import Mesh, PartitionSpec as P

HEAD_DIM = 128
BLOCK = 512


EPSILON = 1e-06


def from_behind(value, axis, by):
    size = lax.axis_size(axis)
    pairs = [(i, i + by) for i in range(size) if 0 <= i + by < size]
    return lax.ppermute(value, axis, pairs)


def exclusive_scan(value, axis):
    size = lax.axis_size(axis)
    pieces = value.reshape(size, -1, value.shape[-1]).astype(jnp.bfloat16)
    gathered = lax.all_to_all(pieces, axis, 0, 0, tiled=True)
    earlier = jnp.arange(size)[:, None] > jnp.arange(size)[None, :]
    before = jnp.dot(
        earlier.astype(gathered.dtype),
        gathered.reshape(size, -1),
        preferred_element_type=jnp.float32,
    ).astype(jnp.bfloat16)
    returned = lax.all_to_all(before.reshape(pieces.shape), axis, 0, 0, tiled=True)
    return returned.reshape(value.shape)


def gather_rows(tokens):
    chips = lax.axis_size("y")
    chip = lax.axis_index("y")
    near = jnp.stack(
        [tokens]
        + [
            lax.ppermute(tokens, "y", [(i, (i - by) % chips) for i in range(chips)])
            for by in range(1, chips)
        ]
    )
    other = lax.ppermute(near, "core", [(0, 1), (1, 0)])
    cores = 2
    both = jnp.concatenate([near, other], axis=0)
    slot = jnp.arange(chips * cores)
    ahead = (slot // cores - chip) % chips
    across = (slot % cores - lax.axis_index("core")) % cores
    ordered = jnp.take(both, across * chips + ahead, axis=0, mode="clip")
    return ordered.reshape(-1, tokens.shape[1])


def body(tokens, w_query, w_key, w_value, norm_gain):
    local_width = w_query.shape[1]
    head_count = local_width // HEAD_DIM
    piece_rows = gather_rows(tokens)
    query_part = jnp.dot(piece_rows, w_query, preferred_element_type=jnp.float32).astype(
        jnp.bfloat16
    )
    key_part = jnp.dot(piece_rows, w_key, preferred_element_type=jnp.float32).astype(jnp.bfloat16)
    value_part = jnp.dot(piece_rows, w_value, preferred_element_type=jnp.float32).astype(
        jnp.bfloat16
    )
    projected = jnp.concatenate([query_part, key_part, value_part], axis=1)
    group_len = projected.shape[0]
    block_count = group_len // BLOCK
    shaped = projected.reshape(block_count, BLOCK, 3, head_count, HEAD_DIM)
    query_rows = shaped[:, :, 0]
    key_rows = shaped[:, :, 1]
    value_rows = shaped[:, :, 2]
    block_states = jnp.einsum(
        "bshd,bshe->bhde", key_rows, value_rows, preferred_element_type=jnp.float32
    )
    local_state = jnp.sum(block_states, axis=0)
    prefix_state = exclusive_scan(local_state, "ctx")
    running = jnp.cumsum(block_states, axis=0)
    earlier = jnp.concatenate([jnp.zeros_like(block_states), running[:-1]], axis=0)
    block_start = (prefix_state.astype(jnp.float32)[None] + earlier).astype(jnp.bfloat16)
    scores = jnp.einsum("bqhd,bkhd->bhqk", query_rows, key_rows, preferred_element_type=jnp.float32)
    causal = jnp.arange(BLOCK)[:, None] >= jnp.arange(BLOCK)[None, :]
    scores = jnp.where(causal[None, None], scores, jnp.float32(0.0)).astype(jnp.bfloat16)
    inner = jnp.einsum("bhqk,bkhe->bqhe", scores, value_rows, preferred_element_type=jnp.float32)
    inner = lax.optimization_barrier(inner)
    carried_part = jnp.einsum(
        "bqhd,bhde->bqhe", query_rows, block_start, preferred_element_type=jnp.float32
    )
    mixed = inner + carried_part
    mean_square = jnp.mean(mixed * mixed, axis=-1, keepdims=True)
    normed = mixed * lax.rsqrt(mean_square + EPSILON) * norm_gain.reshape(head_count, HEAD_DIM)
    return normed.reshape(group_len, local_width).astype(jnp.bfloat16)


def chip_split(mesh):
    first = mesh.devices[0]
    cores = len({getattr(device, "core_on_chip", 0) for device in first})
    return mesh.devices.reshape(mesh.devices.shape[0], -1, cores)


def solution(mesh):
    fine = Mesh(chip_split(mesh), ("ctx", "y", "core"))
    heads = ("y", "core")
    placed = (P(("ctx",) + heads, None), P(None, heads), P(None, heads), P(None, heads), P(heads))
    return jax.shard_map(
        body, mesh=fine, in_specs=placed, out_specs=P("ctx", heads), check_vma=False
    )
```

```python
import jax
import jax.numpy as jnp
from jax import lax
from jax.sharding import Mesh, PartitionSpec as P

HEAD_DIM = 128
BLOCK = 512


EPSILON = 1e-06


def from_behind(value, axis, by):
    size = lax.axis_size(axis)
    pairs = [(i, i + by) for i in range(size) if 0 <= i + by < size]
    return lax.ppermute(value, axis, pairs)


def exclusive_scan(value, axis):
    size = lax.axis_size(axis)
    pieces = value.reshape(size, -1, value.shape[-1]).astype(jnp.bfloat16)
    gathered = lax.all_to_all(pieces, axis, 0, 0, tiled=True)
    earlier = jnp.arange(size)[:, None] > jnp.arange(size)[None, :]
    before = jnp.dot(
        earlier.astype(gathered.dtype),
        gathered.reshape(size, -1),
        preferred_element_type=jnp.float32,
    ).astype(jnp.bfloat16)
    returned = lax.all_to_all(before.reshape(pieces.shape), axis, 0, 0, tiled=True)
    return returned.reshape(value.shape)


def spread(value, axis):
    size = lax.axis_size(axis)
    copies = jnp.broadcast_to(value[None], (size,) + value.shape)
    return lax.all_to_all(copies, axis, 0, 0, tiled=True)


def body(tokens, w_query, w_key, w_value, norm_gain):
    local_width = w_query.shape[1]
    head_count = local_width // HEAD_DIM
    near = spread(tokens, "y")
    other = lax.ppermute(near, "core", [(0, 1), (1, 0)])
    first = lax.axis_index("core") == 0

    def project(weight):
        def half(rows):
            flat = rows.reshape(-1, rows.shape[-1])
            part = jnp.dot(flat, weight, preferred_element_type=jnp.float32).astype(jnp.bfloat16)
            return part.reshape(rows.shape[0], rows.shape[1], weight.shape[1])

        mine, theirs = half(near), half(other)
        paired = jnp.where(
            first, jnp.stack([mine, theirs], axis=1), jnp.stack([theirs, mine], axis=1)
        )
        return paired.reshape(-1, weight.shape[1])

    query_part = project(w_query)
    key_part = project(w_key)
    value_part = project(w_value)
    projected = jnp.concatenate([query_part, key_part, value_part], axis=1)
    group_len = projected.shape[0]
    block_count = group_len // BLOCK
    shaped = projected.reshape(block_count, BLOCK, 3, head_count, HEAD_DIM)
    query_rows = shaped[:, :, 0]
    key_rows = shaped[:, :, 1]
    value_rows = shaped[:, :, 2]
    block_states = jnp.einsum(
        "bshd,bshe->bhde", key_rows, value_rows, preferred_element_type=jnp.float32
    )
    local_state = jnp.sum(block_states, axis=0)
    prefix_state = exclusive_scan(local_state, "ctx")
    running = jnp.cumsum(block_states, axis=0)
    earlier = jnp.concatenate([jnp.zeros_like(block_states), running[:-1]], axis=0)
    block_start = (prefix_state.astype(jnp.float32)[None] + earlier).astype(jnp.bfloat16)
    scores = jnp.einsum("bqhd,bkhd->bhqk", query_rows, key_rows, preferred_element_type=jnp.float32)
    causal = jnp.arange(BLOCK)[:, None] >= jnp.arange(BLOCK)[None, :]
    scores = jnp.where(causal[None, None], scores, jnp.float32(0.0)).astype(jnp.bfloat16)
    inner = jnp.einsum("bhqk,bkhe->bqhe", scores, value_rows, preferred_element_type=jnp.float32)
    inner = lax.optimization_barrier(inner)
    carried_part = jnp.einsum(
        "bqhd,bhde->bqhe", query_rows, block_start, preferred_element_type=jnp.float32
    )
    mixed = inner + carried_part
    mean_square = jnp.mean(mixed * mixed, axis=-1, keepdims=True)
    normed = mixed * lax.rsqrt(mean_square + EPSILON) * norm_gain.reshape(head_count, HEAD_DIM)
    return normed.reshape(group_len, local_width).astype(jnp.bfloat16)


def chip_split(mesh):
    first = mesh.devices[0]
    cores = len({getattr(device, "core_on_chip", 0) for device in first})
    return mesh.devices.reshape(mesh.devices.shape[0], -1, cores)


def solution(mesh):
    fine = Mesh(chip_split(mesh), ("ctx", "y", "core"))
    heads = ("y", "core")
    placed = (P(("ctx",) + heads, None), P(None, heads), P(None, heads), P(None, heads), P(heads))
    return jax.shard_map(
        body, mesh=fine, in_specs=placed, out_specs=P("ctx", heads), check_vma=False
    )
```

```python
import jax
import jax.numpy as jnp
from jax import lax
from jax.experimental import pallas as pl
from jax.sharding import Mesh, PartitionSpec as P

HEAD_DIM = 128
BLOCK = 512


EPSILON = 1e-06


def from_behind(value, axis, by):
    size = lax.axis_size(axis)
    pairs = [(i, i + by) for i in range(size) if 0 <= i + by < size]
    return lax.ppermute(value, axis, pairs)


def exclusive_scan(value, axis):
    size = lax.axis_size(axis)
    pieces = value.reshape(size, -1, value.shape[-1]).astype(jnp.bfloat16)
    gathered = lax.all_to_all(pieces, axis, 0, 0, tiled=True)
    earlier = jnp.arange(size)[:, None] > jnp.arange(size)[None, :]
    before = jnp.dot(
        earlier.astype(gathered.dtype),
        gathered.reshape(size, -1),
        preferred_element_type=jnp.float32,
    ).astype(jnp.bfloat16)
    returned = lax.all_to_all(before.reshape(pieces.shape), axis, 0, 0, tiled=True)
    return returned.reshape(value.shape)


def spread(value, axis):
    size = lax.axis_size(axis)
    copies = jnp.broadcast_to(value[None], (size,) + value.shape)
    return lax.all_to_all(copies, axis, 0, 0, tiled=True)


def gather_rows(tokens):
    near = spread(tokens, "y")
    both = spread(near, "core")
    return both.transpose(1, 0, 2, 3).reshape(-1, tokens.shape[1])


def body(tokens, w_query, w_key, w_value, norm_gain):
    local_width = w_query.shape[1]
    head_count = local_width // HEAD_DIM
    piece_rows = gather_rows(tokens)
    query_part = jnp.dot(piece_rows, w_query, preferred_element_type=jnp.float32).astype(
        jnp.bfloat16
    )
    key_part = jnp.dot(piece_rows, w_key, preferred_element_type=jnp.float32).astype(jnp.bfloat16)
    value_part = jnp.dot(piece_rows, w_value, preferred_element_type=jnp.float32).astype(
        jnp.bfloat16
    )
    projected = jnp.concatenate([query_part, key_part, value_part], axis=1)
    group_len = projected.shape[0]
    block_count = group_len // BLOCK
    shaped = projected.reshape(block_count, BLOCK, 3, head_count, HEAD_DIM)
    query_rows = shaped[:, :, 0]
    key_rows = shaped[:, :, 1]
    value_rows = shaped[:, :, 2]
    block_states = jnp.einsum(
        "bshd,bshe->bhde", key_rows, value_rows, preferred_element_type=jnp.float32
    )
    local_state = jnp.sum(block_states, axis=0)
    prefix_state = exclusive_scan(local_state, "ctx")
    running = jnp.cumsum(block_states, axis=0)
    earlier = jnp.concatenate([jnp.zeros_like(block_states), running[:-1]], axis=0)
    block_start = (prefix_state.astype(jnp.float32)[None] + earlier).astype(jnp.bfloat16)
    scores = jnp.einsum("bqhd,bkhd->bhqk", query_rows, key_rows, preferred_element_type=jnp.float32)
    causal = jnp.arange(BLOCK)[:, None] >= jnp.arange(BLOCK)[None, :]
    scores = jnp.where(causal[None, None], scores, jnp.float32(0.0)).astype(jnp.bfloat16)
    inner = jnp.einsum("bhqk,bkhe->bqhe", scores, value_rows, preferred_element_type=jnp.float32)
    inner = lax.optimization_barrier(inner)
    out = finish(
        query_rows.reshape(group_len, local_width),
        block_start.reshape(block_count * head_count, HEAD_DIM, HEAD_DIM),
        inner.reshape(group_len, local_width),
        norm_gain.reshape(1, local_width),
        head_count,
    )
    return out


def finish_kernel(query_ref, start_ref, inner_ref, gain_ref, out_ref):
    carried = jnp.dot(query_ref[...], start_ref[0], preferred_element_type=jnp.float32)
    mixed = inner_ref[...] + carried
    mean_square = jnp.mean(mixed * mixed, axis=-1, keepdims=True)
    normed = mixed * lax.rsqrt(mean_square + EPSILON) * gain_ref[...]
    out_ref[...] = normed.astype(out_ref.dtype)


def finish(query, start, inner, gain, head_count):
    rows = query.shape[0]
    blocks = rows // BLOCK
    tile = pl.BlockSpec((BLOCK, HEAD_DIM), lambda b, h: (b, h))
    return pl.pallas_call(
        finish_kernel,
        out_shape=jax.ShapeDtypeStruct(query.shape, jnp.bfloat16),
        grid=(blocks, head_count),
        in_specs=[
            tile,
            pl.BlockSpec((1, HEAD_DIM, HEAD_DIM), lambda b, h: (b * head_count + h, 0, 0)),
            tile,
            pl.BlockSpec((1, HEAD_DIM), lambda b, h: (0, h)),
        ],
        out_specs=tile,
    )(query, start, inner, gain)


def chip_split(mesh):
    first = mesh.devices[0]
    cores = len({getattr(device, "core_on_chip", 0) for device in first})
    return mesh.devices.reshape(mesh.devices.shape[0], -1, cores)


def solution(mesh):
    fine = Mesh(chip_split(mesh), ("ctx", "y", "core"))
    heads = ("y", "core")
    placed = (P(("ctx",) + heads, None), P(None, heads), P(None, heads), P(None, heads), P(heads))
    return jax.shard_map(
        body, mesh=fine, in_specs=placed, out_specs=P("ctx", heads), check_vma=False
    )
```

```python
import jax
import jax.numpy as jnp
from jax import lax
from jax.experimental import pallas as pl
from jax.sharding import Mesh, PartitionSpec as P

HEAD_DIM = 128
BLOCK = 512


EPSILON = 1e-06


def from_behind(value, axis, by):
    size = lax.axis_size(axis)
    pairs = [(i, i + by) for i in range(size) if 0 <= i + by < size]
    return lax.ppermute(value, axis, pairs)


def exclusive_scan(value, axis):
    size = lax.axis_size(axis)
    pieces = value.reshape(size, -1, value.shape[-1]).astype(jnp.bfloat16)
    gathered = lax.all_to_all(pieces, axis, 0, 0, tiled=True)
    earlier = jnp.arange(size)[:, None] > jnp.arange(size)[None, :]
    before = jnp.dot(
        earlier.astype(gathered.dtype),
        gathered.reshape(size, -1),
        preferred_element_type=jnp.float32,
    ).astype(jnp.bfloat16)
    returned = lax.all_to_all(before.reshape(pieces.shape), axis, 0, 0, tiled=True)
    return returned.reshape(value.shape)


def spread(value, axis):
    size = lax.axis_size(axis)
    copies = jnp.broadcast_to(value[None], (size,) + value.shape)
    return lax.all_to_all(copies, axis, 0, 0, tiled=True)


def gather_rows(tokens):
    near = spread(tokens, "y")
    both = spread(near, "core")
    return both.transpose(1, 0, 2, 3).reshape(-1, tokens.shape[1])


def body(tokens, w_query, w_key, w_value, norm_gain):
    local_width = w_query.shape[1]
    head_count = local_width // HEAD_DIM
    piece_rows = gather_rows(tokens)
    query_part = jnp.dot(piece_rows, w_query, preferred_element_type=jnp.float32).astype(
        jnp.bfloat16
    )
    key_part = jnp.dot(piece_rows, w_key, preferred_element_type=jnp.float32).astype(jnp.bfloat16)
    value_part = jnp.dot(piece_rows, w_value, preferred_element_type=jnp.float32).astype(
        jnp.bfloat16
    )
    projected = jnp.concatenate([query_part, key_part, value_part], axis=1)
    group_len = projected.shape[0]
    block_count = group_len // BLOCK
    shaped = projected.reshape(block_count, BLOCK, 3, head_count, HEAD_DIM)
    query_rows = shaped[:, :, 0]
    key_rows = shaped[:, :, 1]
    value_rows = shaped[:, :, 2]
    block_states = jnp.einsum(
        "bshd,bshe->bhde", key_rows, value_rows, preferred_element_type=jnp.float32
    )
    local_state = jnp.sum(block_states, axis=0)
    prefix_state = exclusive_scan(local_state, "ctx")
    running = jnp.cumsum(block_states, axis=0)
    earlier = jnp.concatenate([jnp.zeros_like(block_states), running[:-1]], axis=0)
    block_start = (prefix_state.astype(jnp.float32)[None] + earlier).astype(jnp.bfloat16)
    scores = jnp.einsum("bqhd,bkhd->bhqk", query_rows, key_rows, preferred_element_type=jnp.float32)
    causal = jnp.arange(BLOCK)[:, None] >= jnp.arange(BLOCK)[None, :]
    scores = jnp.where(causal[None, None], scores, jnp.float32(0.0)).astype(jnp.bfloat16)
    inner = jnp.einsum("bhqk,bkhe->bqhe", scores, value_rows, preferred_element_type=jnp.float32)
    inner = lax.optimization_barrier(inner)
    out = finish(
        query_rows.reshape(group_len, local_width),
        block_start.reshape(block_count * head_count, HEAD_DIM, HEAD_DIM),
        inner.reshape(group_len, local_width),
        norm_gain.reshape(1, local_width),
        head_count,
    )
    return out


def finish_kernel(query_ref, start_ref, inner_ref, gain_ref, out_ref):
    for head in range(start_ref.shape[0]):
        lanes = slice(head * HEAD_DIM, (head + 1) * HEAD_DIM)
        carried = jnp.dot(
            query_ref[:, lanes], start_ref[head], preferred_element_type=jnp.float32
        )
        mixed = inner_ref[:, lanes] + carried
        mean_square = jnp.mean(mixed * mixed, axis=-1, keepdims=True)
        normed = mixed * lax.rsqrt(mean_square + EPSILON) * gain_ref[:, lanes]
        out_ref[:, lanes] = normed.astype(out_ref.dtype)


def finish(query, start, inner, gain, head_count):
    rows, width = query.shape
    blocks = rows // BLOCK
    tile = pl.BlockSpec((BLOCK, width), lambda b: (b, 0))
    return pl.pallas_call(
        finish_kernel,
        out_shape=jax.ShapeDtypeStruct(query.shape, jnp.bfloat16),
        grid=(blocks,),
        in_specs=[
            tile,
            pl.BlockSpec((head_count, HEAD_DIM, HEAD_DIM), lambda b: (b, 0, 0)),
            tile,
            pl.BlockSpec((1, width), lambda b: (0, 0)),
        ],
        out_specs=tile,
    )(query, start, inner, gain)


def chip_split(mesh):
    first = mesh.devices[0]
    cores = len({getattr(device, "core_on_chip", 0) for device in first})
    return mesh.devices.reshape(mesh.devices.shape[0], -1, cores)


def solution(mesh):
    fine = Mesh(chip_split(mesh), ("ctx", "y", "core"))
    heads = ("y", "core")
    placed = (P(("ctx",) + heads, None), P(None, heads), P(None, heads), P(None, heads), P(heads))
    return jax.shard_map(
        body, mesh=fine, in_specs=placed, out_specs=P("ctx", heads), check_vma=False
    )
```

```python
import jax
import jax.numpy as jnp
from jax import lax
from jax.experimental import pallas as pl
from jax.sharding import Mesh, PartitionSpec as P

HEAD_DIM = 128
BLOCK = 512


EPSILON = 1e-06


def from_behind(value, axis, by):
    size = lax.axis_size(axis)
    pairs = [(i, i + by) for i in range(size) if 0 <= i + by < size]
    return lax.ppermute(value, axis, pairs)


def exclusive_scan(value, axis):
    size = lax.axis_size(axis)
    pieces = value.reshape(size, -1, value.shape[-1]).astype(jnp.bfloat16)
    gathered = lax.all_to_all(pieces, axis, 0, 0, tiled=True)
    earlier = jnp.arange(size)[:, None] > jnp.arange(size)[None, :]
    before = jnp.dot(
        earlier.astype(gathered.dtype),
        gathered.reshape(size, -1),
        preferred_element_type=jnp.float32,
    ).astype(jnp.bfloat16)
    returned = lax.all_to_all(before.reshape(pieces.shape), axis, 0, 0, tiled=True)
    return returned.reshape(value.shape)


def spread(value, axis):
    size = lax.axis_size(axis)
    copies = jnp.broadcast_to(value[None], (size,) + value.shape)
    return lax.all_to_all(copies, axis, 0, 0, tiled=True)


def gather_rows(tokens):
    near = spread(tokens, "y")
    both = spread(near, "core")
    return both.transpose(1, 0, 2, 3).reshape(-1, tokens.shape[1])


def body(tokens, w_query, w_key, w_value, norm_gain):
    local_width = w_query.shape[1]
    head_count = local_width // HEAD_DIM
    piece_rows = gather_rows(tokens)
    query_part = jnp.dot(piece_rows, w_query, preferred_element_type=jnp.float32).astype(
        jnp.bfloat16
    )
    key_part = jnp.dot(piece_rows, w_key, preferred_element_type=jnp.float32).astype(jnp.bfloat16)
    value_part = jnp.dot(piece_rows, w_value, preferred_element_type=jnp.float32).astype(
        jnp.bfloat16
    )
    group_len = query_part.shape[0]
    block_count = group_len // BLOCK
    query_rows, key_rows, value_rows = (
        part.reshape(block_count, BLOCK, head_count, HEAD_DIM)
        for part in (query_part, key_part, value_part)
    )
    block_states = jnp.einsum(
        "bshd,bshe->bhde", key_rows, value_rows, preferred_element_type=jnp.float32
    )
    local_state = jnp.sum(block_states, axis=0)
    prefix_state = exclusive_scan(local_state, "ctx")
    running = jnp.cumsum(block_states, axis=0)
    earlier = jnp.concatenate([jnp.zeros_like(block_states), running[:-1]], axis=0)
    block_start = (prefix_state.astype(jnp.float32)[None] + earlier).astype(jnp.bfloat16)
    scores = jnp.einsum("bqhd,bkhd->bhqk", query_rows, key_rows, preferred_element_type=jnp.float32)
    causal = jnp.arange(BLOCK)[:, None] >= jnp.arange(BLOCK)[None, :]
    scores = jnp.where(causal[None, None], scores, jnp.float32(0.0)).astype(jnp.bfloat16)
    inner = jnp.einsum("bhqk,bkhe->bqhe", scores, value_rows, preferred_element_type=jnp.float32)
    inner = lax.optimization_barrier(inner)
    out = finish(
        query_rows.reshape(group_len, local_width),
        block_start.reshape(block_count * head_count, HEAD_DIM, HEAD_DIM),
        inner.reshape(group_len, local_width),
        norm_gain.reshape(1, local_width),
        head_count,
    )
    return out


def finish_kernel(query_ref, start_ref, inner_ref, gain_ref, out_ref):
    for head in range(start_ref.shape[0]):
        lanes = slice(head * HEAD_DIM, (head + 1) * HEAD_DIM)
        carried = jnp.dot(
            query_ref[:, lanes], start_ref[head], preferred_element_type=jnp.float32
        )
        mixed = inner_ref[:, lanes] + carried
        mean_square = jnp.mean(mixed * mixed, axis=-1, keepdims=True)
        normed = mixed * lax.rsqrt(mean_square + EPSILON) * gain_ref[:, lanes]
        out_ref[:, lanes] = normed.astype(out_ref.dtype)


def finish(query, start, inner, gain, head_count):
    rows, width = query.shape
    blocks = rows // BLOCK
    tile = pl.BlockSpec((BLOCK, width), lambda b: (b, 0))
    return pl.pallas_call(
        finish_kernel,
        out_shape=jax.ShapeDtypeStruct(query.shape, jnp.bfloat16),
        grid=(blocks,),
        in_specs=[
            tile,
            pl.BlockSpec((head_count, HEAD_DIM, HEAD_DIM), lambda b: (b, 0, 0)),
            tile,
            pl.BlockSpec((1, width), lambda b: (0, 0)),
        ],
        out_specs=tile,
    )(query, start, inner, gain)


def chip_split(mesh):
    first = mesh.devices[0]
    cores = len({getattr(device, "core_on_chip", 0) for device in first})
    return mesh.devices.reshape(mesh.devices.shape[0], -1, cores)


def solution(mesh):
    fine = Mesh(chip_split(mesh), ("ctx", "y", "core"))
    heads = ("y", "core")
    placed = (P(("ctx",) + heads, None), P(None, heads), P(None, heads), P(None, heads), P(heads))
    return jax.shard_map(
        body, mesh=fine, in_specs=placed, out_specs=P("ctx", heads), check_vma=False
    )
```

```python
import jax
import jax.numpy as jnp
from jax import lax
from jax.experimental import pallas as pl
from jax.sharding import Mesh, PartitionSpec as P

HEAD_DIM = 128
BLOCK = 512


EPSILON = 1e-06


def from_behind(value, axis, by):
    size = lax.axis_size(axis)
    pairs = [(i, i + by) for i in range(size) if 0 <= i + by < size]
    return lax.ppermute(value, axis, pairs)


def exclusive_scan(value, axis):
    size = lax.axis_size(axis)
    pieces = value.reshape(size, -1, value.shape[-1]).astype(jnp.bfloat16)
    gathered = lax.all_to_all(pieces, axis, 0, 0, tiled=True)
    earlier = jnp.arange(size)[:, None] > jnp.arange(size)[None, :]
    before = jnp.dot(
        earlier.astype(gathered.dtype),
        gathered.reshape(size, -1),
        preferred_element_type=jnp.float32,
    ).astype(jnp.bfloat16)
    returned = lax.all_to_all(before.reshape(pieces.shape), axis, 0, 0, tiled=True)
    return returned.reshape(value.shape)


def spread(value, axis):
    size = lax.axis_size(axis)
    copies = jnp.broadcast_to(value[None], (size,) + value.shape)
    return lax.all_to_all(copies, axis, 0, 0, tiled=True)


def gather_rows(tokens):
    near = spread(tokens, "y")
    both = spread(near, "core")
    return both.transpose(1, 0, 2, 3).reshape(-1, tokens.shape[1])


def body(tokens, w_query, w_key, w_value, norm_gain):
    local_width = w_query.shape[1]
    head_count = local_width // HEAD_DIM
    piece_rows = gather_rows(tokens)
    query_part = jnp.dot(piece_rows, w_query, preferred_element_type=jnp.float32).astype(
        jnp.bfloat16
    )
    key_part = jnp.dot(piece_rows, w_key, preferred_element_type=jnp.float32).astype(jnp.bfloat16)
    value_part = jnp.dot(piece_rows, w_value, preferred_element_type=jnp.float32).astype(
        jnp.bfloat16
    )
    group_len = query_part.shape[0]
    block_count = group_len // BLOCK
    query_rows, key_rows, value_rows = (
        part.reshape(block_count, BLOCK, head_count, HEAD_DIM)
        for part in (query_part, key_part, value_part)
    )
    block_states = jnp.einsum(
        "bshd,bshe->bhde", key_rows, value_rows, preferred_element_type=jnp.float32
    )
    local_state = jnp.sum(block_states, axis=0)
    prefix_state = exclusive_scan(local_state, "ctx")
    running = jnp.cumsum(block_states, axis=0)
    earlier = jnp.concatenate([jnp.zeros_like(block_states), running[:-1]], axis=0)
    block_start = (prefix_state.astype(jnp.float32)[None] + earlier).astype(jnp.bfloat16)
    scores = jnp.einsum("bqhd,bkhd->bhqk", query_rows, key_rows, preferred_element_type=jnp.float32)
    causal = lax.broadcasted_iota(jnp.int32, scores.shape, 2) >= lax.broadcasted_iota(
        jnp.int32, scores.shape, 3
    )
    scores = jnp.where(causal, scores, jnp.float32(0.0)).astype(jnp.bfloat16)
    inner = jnp.einsum("bhqk,bkhe->bqhe", scores, value_rows, preferred_element_type=jnp.float32)
    inner = lax.optimization_barrier(inner)
    out = finish(
        query_rows.reshape(group_len, local_width),
        block_start.reshape(block_count * head_count, HEAD_DIM, HEAD_DIM),
        inner.reshape(group_len, local_width),
        norm_gain.reshape(1, local_width),
        head_count,
    )
    return out


def finish_kernel(query_ref, start_ref, inner_ref, gain_ref, out_ref):
    for head in range(start_ref.shape[0]):
        lanes = slice(head * HEAD_DIM, (head + 1) * HEAD_DIM)
        carried = jnp.dot(
            query_ref[:, lanes], start_ref[head], preferred_element_type=jnp.float32
        )
        mixed = inner_ref[:, lanes] + carried
        mean_square = jnp.mean(mixed * mixed, axis=-1, keepdims=True)
        normed = mixed * lax.rsqrt(mean_square + EPSILON) * gain_ref[:, lanes]
        out_ref[:, lanes] = normed.astype(out_ref.dtype)


def finish(query, start, inner, gain, head_count):
    rows, width = query.shape
    blocks = rows // BLOCK
    tile = pl.BlockSpec((BLOCK, width), lambda b: (b, 0))
    return pl.pallas_call(
        finish_kernel,
        out_shape=jax.ShapeDtypeStruct(query.shape, jnp.bfloat16),
        grid=(blocks,),
        in_specs=[
            tile,
            pl.BlockSpec((head_count, HEAD_DIM, HEAD_DIM), lambda b: (b, 0, 0)),
            tile,
            pl.BlockSpec((1, width), lambda b: (0, 0)),
        ],
        out_specs=tile,
    )(query, start, inner, gain)


def chip_split(mesh):
    first = mesh.devices[0]
    cores = len({getattr(device, "core_on_chip", 0) for device in first})
    return mesh.devices.reshape(mesh.devices.shape[0], -1, cores)


def solution(mesh):
    fine = Mesh(chip_split(mesh), ("ctx", "y", "core"))
    heads = ("y", "core")
    placed = (P(("ctx",) + heads, None), P(None, heads), P(None, heads), P(None, heads), P(heads))
    return jax.shard_map(
        body, mesh=fine, in_specs=placed, out_specs=P("ctx", heads), check_vma=False
    )
```

```python
import jax
import jax.numpy as jnp
from jax import lax
from jax.experimental import pallas as pl
from jax.sharding import Mesh, PartitionSpec as P

HEAD_DIM = 128
BLOCK = 512


EPSILON = 1e-06


def from_behind(value, axis, by):
    size = lax.axis_size(axis)
    pairs = [(i, i + by) for i in range(size) if 0 <= i + by < size]
    return lax.ppermute(value, axis, pairs)


def exclusive_scan(value, axis):
    size = lax.axis_size(axis)
    pieces = value.reshape(size, -1, value.shape[-1]).astype(jnp.bfloat16)
    gathered = lax.all_to_all(pieces, axis, 0, 0, tiled=True)
    earlier = jnp.arange(size)[:, None] > jnp.arange(size)[None, :]
    before = jnp.dot(
        earlier.astype(gathered.dtype),
        gathered.reshape(size, -1),
        preferred_element_type=jnp.float32,
    ).astype(jnp.bfloat16)
    returned = lax.all_to_all(before.reshape(pieces.shape), axis, 0, 0, tiled=True)
    return returned.reshape(value.shape)


def spread(value, axis):
    size = lax.axis_size(axis)
    copies = jnp.broadcast_to(value[None], (size,) + value.shape)
    return lax.all_to_all(copies, axis, 0, 0, tiled=True)


def gather_rows(tokens):
    near = spread(tokens, "y")
    other = lax.ppermute(near, "core", [(0, 1), (1, 0)])
    both = jnp.where(
        lax.axis_index("core") == 0, jnp.stack([near, other]), jnp.stack([other, near])
    )
    return both.transpose(1, 0, 2, 3).reshape(-1, tokens.shape[1])


def body(tokens, w_query, w_key, w_value, norm_gain):
    local_width = w_query.shape[1]
    head_count = local_width // HEAD_DIM
    piece_rows = gather_rows(tokens)
    query_part = jnp.dot(piece_rows, w_query, preferred_element_type=jnp.float32).astype(
        jnp.bfloat16
    )
    key_part = jnp.dot(piece_rows, w_key, preferred_element_type=jnp.float32).astype(jnp.bfloat16)
    value_part = jnp.dot(piece_rows, w_value, preferred_element_type=jnp.float32).astype(
        jnp.bfloat16
    )
    group_len = query_part.shape[0]
    block_count = group_len // BLOCK
    query_rows, key_rows, value_rows = (
        part.reshape(block_count, BLOCK, head_count, HEAD_DIM)
        for part in (query_part, key_part, value_part)
    )
    block_states = jnp.einsum(
        "bshd,bshe->bhde", key_rows, value_rows, preferred_element_type=jnp.float32
    )
    local_state = jnp.sum(block_states, axis=0)
    prefix_state = exclusive_scan(local_state, "ctx")
    running = jnp.cumsum(block_states, axis=0)
    earlier = jnp.concatenate([jnp.zeros_like(block_states), running[:-1]], axis=0)
    block_start = (prefix_state.astype(jnp.float32)[None] + earlier).astype(jnp.bfloat16)
    scores = jnp.einsum("bqhd,bkhd->bhqk", query_rows, key_rows, preferred_element_type=jnp.float32)
    causal = lax.broadcasted_iota(jnp.int32, scores.shape, 2) >= lax.broadcasted_iota(
        jnp.int32, scores.shape, 3
    )
    scores = jnp.where(causal, scores, jnp.float32(0.0)).astype(jnp.bfloat16)
    inner = jnp.einsum("bhqk,bkhe->bqhe", scores, value_rows, preferred_element_type=jnp.float32)
    inner = lax.optimization_barrier(inner)
    out = finish(
        query_rows.reshape(group_len, local_width),
        block_start.reshape(block_count * head_count, HEAD_DIM, HEAD_DIM),
        inner.reshape(group_len, local_width),
        norm_gain.reshape(1, local_width),
        head_count,
    )
    return out


def finish_kernel(query_ref, start_ref, inner_ref, gain_ref, out_ref):
    for head in range(start_ref.shape[0]):
        lanes = slice(head * HEAD_DIM, (head + 1) * HEAD_DIM)
        carried = jnp.dot(
            query_ref[:, lanes], start_ref[head], preferred_element_type=jnp.float32
        )
        mixed = inner_ref[:, lanes] + carried
        mean_square = jnp.mean(mixed * mixed, axis=-1, keepdims=True)
        normed = mixed * lax.rsqrt(mean_square + EPSILON) * gain_ref[:, lanes]
        out_ref[:, lanes] = normed.astype(out_ref.dtype)


def finish(query, start, inner, gain, head_count):
    rows, width = query.shape
    blocks = rows // BLOCK
    tile = pl.BlockSpec((BLOCK, width), lambda b: (b, 0))
    return pl.pallas_call(
        finish_kernel,
        out_shape=jax.ShapeDtypeStruct(query.shape, jnp.bfloat16),
        grid=(blocks,),
        in_specs=[
            tile,
            pl.BlockSpec((head_count, HEAD_DIM, HEAD_DIM), lambda b: (b, 0, 0)),
            tile,
            pl.BlockSpec((1, width), lambda b: (0, 0)),
        ],
        out_specs=tile,
    )(query, start, inner, gain)


def chip_split(mesh):
    first = mesh.devices[0]
    cores = len({getattr(device, "core_on_chip", 0) for device in first})
    return mesh.devices.reshape(mesh.devices.shape[0], -1, cores)


def solution(mesh):
    fine = Mesh(chip_split(mesh), ("ctx", "y", "core"))
    heads = ("y", "core")
    placed = (P(("ctx",) + heads, None), P(None, heads), P(None, heads), P(None, heads), P(heads))
    return jax.shard_map(
        body, mesh=fine, in_specs=placed, out_specs=P("ctx", heads), check_vma=False
    )
```

```python
import jax
import jax.numpy as jnp
from jax import lax
from jax.experimental import pallas as pl
from jax.sharding import Mesh, PartitionSpec as P

HEAD_DIM = 128
BLOCK = 512


EPSILON = 1e-06


def from_behind(value, axis, by):
    size = lax.axis_size(axis)
    pairs = [(i, i + by) for i in range(size) if 0 <= i + by < size]
    return lax.ppermute(value, axis, pairs)


def exclusive_scan(value, axis):
    size = lax.axis_size(axis)
    pieces = value.reshape(size, -1, value.shape[-1]).astype(jnp.bfloat16)
    gathered = lax.all_to_all(pieces, axis, 0, 0, tiled=True)
    wide = gathered.astype(jnp.float32)
    total = jnp.zeros_like(wide[0])
    partial = []
    for source in range(size):
        partial.append(total)
        total = total + wide[source]
    before = jnp.stack(partial).astype(jnp.bfloat16)
    returned = lax.all_to_all(before, axis, 0, 0, tiled=True)
    return returned.reshape(value.shape)


def spread(value, axis):
    size = lax.axis_size(axis)
    copies = jnp.broadcast_to(value[None], (size,) + value.shape)
    return lax.all_to_all(copies, axis, 0, 0, tiled=True)


def gather_rows(tokens):
    near = spread(tokens, "y")
    both = spread(near, "core")
    return both.transpose(1, 0, 2, 3).reshape(-1, tokens.shape[1])


def body(tokens, w_query, w_key, w_value, norm_gain):
    local_width = w_query.shape[1]
    head_count = local_width // HEAD_DIM
    piece_rows = gather_rows(tokens)
    query_part = jnp.dot(piece_rows, w_query, preferred_element_type=jnp.float32).astype(
        jnp.bfloat16
    )
    key_part = jnp.dot(piece_rows, w_key, preferred_element_type=jnp.float32).astype(jnp.bfloat16)
    value_part = jnp.dot(piece_rows, w_value, preferred_element_type=jnp.float32).astype(
        jnp.bfloat16
    )
    group_len = query_part.shape[0]
    block_count = group_len // BLOCK
    query_rows, key_rows, value_rows = (
        part.reshape(block_count, BLOCK, head_count, HEAD_DIM)
        for part in (query_part, key_part, value_part)
    )
    block_states = jnp.einsum(
        "bshd,bshe->bhde", key_rows, value_rows, preferred_element_type=jnp.float32
    )
    local_state = jnp.sum(block_states, axis=0)
    prefix_state = exclusive_scan(local_state, "ctx")
    running = jnp.cumsum(block_states, axis=0)
    earlier = jnp.concatenate([jnp.zeros_like(block_states), running[:-1]], axis=0)
    block_start = (prefix_state.astype(jnp.float32)[None] + earlier).astype(jnp.bfloat16)
    scores = jnp.einsum("bqhd,bkhd->bhqk", query_rows, key_rows, preferred_element_type=jnp.float32)
    causal = lax.broadcasted_iota(jnp.int32, scores.shape, 2) >= lax.broadcasted_iota(
        jnp.int32, scores.shape, 3
    )
    scores = jnp.where(causal, scores, jnp.float32(0.0)).astype(jnp.bfloat16)
    inner = jnp.einsum("bhqk,bkhe->bqhe", scores, value_rows, preferred_element_type=jnp.float32)
    inner = lax.optimization_barrier(inner)
    out = finish(
        query_rows.reshape(group_len, local_width),
        block_start.reshape(block_count * head_count, HEAD_DIM, HEAD_DIM),
        inner.reshape(group_len, local_width),
        norm_gain.reshape(1, local_width),
        head_count,
    )
    return out


def finish_kernel(query_ref, start_ref, inner_ref, gain_ref, out_ref):
    for head in range(start_ref.shape[0]):
        lanes = slice(head * HEAD_DIM, (head + 1) * HEAD_DIM)
        carried = jnp.dot(
            query_ref[:, lanes], start_ref[head], preferred_element_type=jnp.float32
        )
        mixed = inner_ref[:, lanes] + carried
        mean_square = jnp.mean(mixed * mixed, axis=-1, keepdims=True)
        normed = mixed * lax.rsqrt(mean_square + EPSILON) * gain_ref[:, lanes]
        out_ref[:, lanes] = normed.astype(out_ref.dtype)


def finish(query, start, inner, gain, head_count):
    rows, width = query.shape
    blocks = rows // BLOCK
    tile = pl.BlockSpec((BLOCK, width), lambda b: (b, 0))
    return pl.pallas_call(
        finish_kernel,
        out_shape=jax.ShapeDtypeStruct(query.shape, jnp.bfloat16),
        grid=(blocks,),
        in_specs=[
            tile,
            pl.BlockSpec((head_count, HEAD_DIM, HEAD_DIM), lambda b: (b, 0, 0)),
            tile,
            pl.BlockSpec((1, width), lambda b: (0, 0)),
        ],
        out_specs=tile,
    )(query, start, inner, gain)


def chip_split(mesh):
    first = mesh.devices[0]
    cores = len({getattr(device, "core_on_chip", 0) for device in first})
    return mesh.devices.reshape(mesh.devices.shape[0], -1, cores)


def solution(mesh):
    fine = Mesh(chip_split(mesh), ("ctx", "y", "core"))
    heads = ("y", "core")
    placed = (P(("ctx",) + heads, None), P(None, heads), P(None, heads), P(None, heads), P(heads))
    return jax.shard_map(
        body, mesh=fine, in_specs=placed, out_specs=P("ctx", heads), check_vma=False
    )
```

```python
import jax
import jax.numpy as jnp
from jax import lax
from jax.experimental import pallas as pl
from jax.sharding import Mesh, PartitionSpec as P

HEAD_DIM = 128
BLOCK = 512


EPSILON = 1e-06


def from_behind(value, axis, by):
    size = lax.axis_size(axis)
    pairs = [(i, i + by) for i in range(size) if 0 <= i + by < size]
    return lax.ppermute(value, axis, pairs)


def exclusive_scan(value, axis):
    size = lax.axis_size(axis)
    pieces = value.reshape(size, -1, value.shape[-1]).astype(jnp.bfloat16)
    gathered = lax.all_to_all(pieces, axis, 0, 0, tiled=True)
    earlier = jnp.arange(size)[:, None] > jnp.arange(size)[None, :]
    before = jnp.dot(
        earlier.astype(gathered.dtype),
        gathered.reshape(size, -1),
        preferred_element_type=jnp.float32,
    ).astype(jnp.bfloat16)
    returned = lax.all_to_all(before.reshape(pieces.shape), axis, 0, 0, tiled=True)
    return returned.reshape(value.shape)


def spread(value, axis):
    size = lax.axis_size(axis)
    copies = jnp.broadcast_to(value[None], (size,) + value.shape)
    return lax.all_to_all(copies, axis, 0, 0, tiled=True)


def gather_rows(tokens):
    near = spread(tokens, "y")
    both = spread(near, "core")
    return both.transpose(1, 0, 2, 3).reshape(-1, tokens.shape[1])


def body(tokens, w_query, w_key, w_value, norm_gain):
    local_width = w_query.shape[1]
    head_count = local_width // HEAD_DIM
    piece_rows = gather_rows(tokens)
    query_part = jnp.dot(piece_rows, w_query, preferred_element_type=jnp.float32).astype(
        jnp.bfloat16
    )
    key_part = jnp.dot(piece_rows, w_key, preferred_element_type=jnp.float32).astype(jnp.bfloat16)
    value_part = jnp.dot(piece_rows, w_value, preferred_element_type=jnp.float32).astype(
        jnp.bfloat16
    )
    group_len = query_part.shape[0]
    block_count = group_len // BLOCK
    query_rows, key_rows, value_rows = (
        part.reshape(block_count, BLOCK, head_count, HEAD_DIM)
        for part in (query_part, key_part, value_part)
    )
    block_states = jnp.einsum(
        "bshd,bshe->bhde", key_rows, value_rows, preferred_element_type=jnp.float32
    )
    local_state = jnp.sum(block_states, axis=0)
    prefix_state = exclusive_scan(local_state, "ctx")
    running = jnp.cumsum(block_states, axis=0)
    earlier = jnp.concatenate([jnp.zeros_like(block_states), running[:-1]], axis=0)
    block_start = (prefix_state.astype(jnp.float32)[None] + earlier).astype(jnp.bfloat16)
    scores = jnp.einsum("bqhd,bkhd->bhqk", query_rows, key_rows, preferred_element_type=jnp.float32)
    causal = lax.broadcasted_iota(jnp.int32, scores.shape, 2) >= lax.broadcasted_iota(
        jnp.int32, scores.shape, 3
    )
    scores = jnp.where(causal, scores, jnp.float32(0.0)).astype(jnp.bfloat16)
    inner = jnp.einsum("bhqk,bkhe->bqhe", scores, value_rows, preferred_element_type=jnp.float32)
    inner = lax.optimization_barrier(inner)
    out = finish(
        query_rows.reshape(group_len, local_width),
        block_start.reshape(block_count * head_count, HEAD_DIM, HEAD_DIM),
        inner.reshape(group_len, local_width),
        norm_gain.reshape(1, local_width),
        head_count,
    )
    return out


def finish_kernel(query_ref, start_ref, inner_ref, gain_ref, out_ref):
    for head in range(start_ref.shape[0]):
        lanes = slice(head * HEAD_DIM, (head + 1) * HEAD_DIM)
        carried = jnp.dot(
            query_ref[:, lanes], start_ref[head], preferred_element_type=jnp.float32
        )
        mixed = inner_ref[:, lanes] + carried
        mean_square = jnp.mean(mixed * mixed, axis=-1, keepdims=True)
        normed = mixed * lax.rsqrt(mean_square + EPSILON) * gain_ref[:, lanes]
        out_ref[:, lanes] = normed.astype(out_ref.dtype)


def finish(query, start, inner, gain, head_count):
    rows, width = query.shape
    blocks = rows // BLOCK
    parts = 2 if head_count % 2 == 0 else 1
    group = head_count // parts
    tile = pl.BlockSpec((BLOCK, group * HEAD_DIM), lambda b, p: (b, p))
    return pl.pallas_call(
        finish_kernel,
        out_shape=jax.ShapeDtypeStruct(query.shape, jnp.bfloat16),
        grid=(blocks, parts),
        in_specs=[
            tile,
            pl.BlockSpec((group, HEAD_DIM, HEAD_DIM), lambda b, p: (b * parts + p, 0, 0)),
            tile,
            pl.BlockSpec((1, group * HEAD_DIM), lambda b, p: (0, p)),
        ],
        out_specs=tile,
    )(query, start, inner, gain)


def chip_split(mesh):
    first = mesh.devices[0]
    cores = len({getattr(device, "core_on_chip", 0) for device in first})
    return mesh.devices.reshape(mesh.devices.shape[0], -1, cores)


def solution(mesh):
    fine = Mesh(chip_split(mesh), ("ctx", "y", "core"))
    heads = ("y", "core")
    placed = (P(("ctx",) + heads, None), P(None, heads), P(None, heads), P(None, heads), P(heads))
    return jax.shard_map(
        body, mesh=fine, in_specs=placed, out_specs=P("ctx", heads), check_vma=False
    )
```

```python
import jax
import jax.numpy as jnp
from jax import lax
from jax.experimental import pallas as pl
from jax.sharding import Mesh, PartitionSpec as P

HEAD_DIM = 128
BLOCK = 512


EPSILON = 1e-06


def from_behind(value, axis, by):
    size = lax.axis_size(axis)
    pairs = [(i, i + by) for i in range(size) if 0 <= i + by < size]
    return lax.ppermute(value, axis, pairs)


def exclusive_scan(value, axis):
    size = lax.axis_size(axis)
    pieces = value.reshape(size, -1, value.shape[-1]).astype(jnp.bfloat16)
    gathered = lax.all_to_all(pieces, axis, 0, 0, tiled=True)
    earlier = jnp.arange(size)[:, None] > jnp.arange(size)[None, :]
    before = jnp.dot(
        earlier.astype(gathered.dtype),
        gathered.reshape(size, -1),
        preferred_element_type=jnp.float32,
    ).astype(jnp.bfloat16)
    returned = lax.all_to_all(before.reshape(pieces.shape), axis, 0, 0, tiled=True)
    return returned.reshape(value.shape)


def spread(value, axis):
    size = lax.axis_size(axis)
    copies = jnp.broadcast_to(value[None], (size,) + value.shape)
    return lax.all_to_all(copies, axis, 0, 0, tiled=True)


def gather_rows(tokens):
    near = spread(tokens, "y")
    both = spread(near, "core")
    return both.transpose(1, 0, 2, 3).reshape(-1, tokens.shape[1])


def body(tokens, w_query, w_key, w_value, norm_gain):
    local_width = w_query.shape[1]
    head_count = local_width // HEAD_DIM
    piece_rows = gather_rows(tokens)
    query_part = jnp.dot(piece_rows, w_query, preferred_element_type=jnp.float32).astype(
        jnp.bfloat16
    )
    key_part = jnp.dot(piece_rows, w_key, preferred_element_type=jnp.float32).astype(jnp.bfloat16)
    value_part = jnp.dot(piece_rows, w_value, preferred_element_type=jnp.float32).astype(
        jnp.bfloat16
    )
    group_len = query_part.shape[0]
    block_count = group_len // BLOCK
    query_rows, key_rows, value_rows = (
        part.reshape(block_count, BLOCK, head_count, HEAD_DIM)
        for part in (query_part, key_part, value_part)
    )
    block_states = jnp.einsum(
        "bshd,bshe->bhde", key_rows, value_rows, preferred_element_type=jnp.float32
    )
    local_state = jnp.sum(block_states, axis=0)
    local_state, query_rows = lax.optimization_barrier((local_state, query_rows))
    prefix_state = exclusive_scan(local_state, "ctx")
    running = jnp.cumsum(block_states, axis=0)
    earlier = jnp.concatenate([jnp.zeros_like(block_states), running[:-1]], axis=0)
    block_start = (prefix_state.astype(jnp.float32)[None] + earlier).astype(jnp.bfloat16)
    scores = jnp.einsum("bqhd,bkhd->bhqk", query_rows, key_rows, preferred_element_type=jnp.float32)
    causal = lax.broadcasted_iota(jnp.int32, scores.shape, 2) >= lax.broadcasted_iota(
        jnp.int32, scores.shape, 3
    )
    scores = jnp.where(causal, scores, jnp.float32(0.0)).astype(jnp.bfloat16)
    inner = jnp.einsum("bhqk,bkhe->bqhe", scores, value_rows, preferred_element_type=jnp.float32)
    inner = lax.optimization_barrier(inner)
    out = finish(
        query_rows.reshape(group_len, local_width),
        block_start.reshape(block_count * head_count, HEAD_DIM, HEAD_DIM),
        inner.reshape(group_len, local_width),
        norm_gain.reshape(1, local_width),
        head_count,
    )
    return out


def finish_kernel(query_ref, start_ref, inner_ref, gain_ref, out_ref):
    for head in range(start_ref.shape[0]):
        lanes = slice(head * HEAD_DIM, (head + 1) * HEAD_DIM)
        carried = jnp.dot(
            query_ref[:, lanes], start_ref[head], preferred_element_type=jnp.float32
        )
        mixed = inner_ref[:, lanes] + carried
        mean_square = jnp.mean(mixed * mixed, axis=-1, keepdims=True)
        normed = mixed * lax.rsqrt(mean_square + EPSILON) * gain_ref[:, lanes]
        out_ref[:, lanes] = normed.astype(out_ref.dtype)


def finish(query, start, inner, gain, head_count):
    rows, width = query.shape
    blocks = rows // BLOCK
    tile = pl.BlockSpec((BLOCK, width), lambda b: (b, 0))
    return pl.pallas_call(
        finish_kernel,
        out_shape=jax.ShapeDtypeStruct(query.shape, jnp.bfloat16),
        grid=(blocks,),
        in_specs=[
            tile,
            pl.BlockSpec((head_count, HEAD_DIM, HEAD_DIM), lambda b: (b, 0, 0)),
            tile,
            pl.BlockSpec((1, width), lambda b: (0, 0)),
        ],
        out_specs=tile,
    )(query, start, inner, gain)


def chip_split(mesh):
    first = mesh.devices[0]
    cores = len({getattr(device, "core_on_chip", 0) for device in first})
    return mesh.devices.reshape(mesh.devices.shape[0], -1, cores)


def solution(mesh):
    fine = Mesh(chip_split(mesh), ("ctx", "y", "core"))
    heads = ("y", "core")
    placed = (P(("ctx",) + heads, None), P(None, heads), P(None, heads), P(None, heads), P(heads))
    return jax.shard_map(
        body, mesh=fine, in_specs=placed, out_specs=P("ctx", heads), check_vma=False
    )
```

```python
import jax
import jax.numpy as jnp
from jax import lax
from jax.experimental import pallas as pl
from jax.sharding import Mesh, PartitionSpec as P

HEAD_DIM = 128
BLOCK = 512


EPSILON = 1e-06


def from_behind(value, axis, by):
    size = lax.axis_size(axis)
    pairs = [(i, i + by) for i in range(size) if 0 <= i + by < size]
    return lax.ppermute(value, axis, pairs)


def exclusive_scan(value, axis):
    size = lax.axis_size(axis)
    pieces = value.reshape(size, -1, value.shape[-1]).astype(jnp.bfloat16)
    gathered = lax.all_to_all(pieces, axis, 0, 0, tiled=True)
    earlier = jnp.arange(size)[:, None] > jnp.arange(size)[None, :]
    before = jnp.dot(
        earlier.astype(gathered.dtype),
        gathered.reshape(size, -1),
        preferred_element_type=jnp.float32,
    ).astype(jnp.bfloat16)
    returned = lax.all_to_all(before.reshape(pieces.shape), axis, 0, 0, tiled=True)
    return returned.reshape(value.shape)


def spread(value, axis):
    size = lax.axis_size(axis)
    copies = jnp.broadcast_to(value[None], (size,) + value.shape)
    return lax.all_to_all(copies, axis, 0, 0, tiled=True)


def gather_rows(tokens):
    near = spread(tokens, "y")
    both = spread(near, "core")
    return both.transpose(1, 0, 2, 3).reshape(-1, tokens.shape[1])


def body(tokens, w_query, w_key, w_value, norm_gain):
    local_width = w_query.shape[1]
    head_count = local_width // HEAD_DIM
    piece_rows = gather_rows(tokens)
    query_part = jnp.dot(piece_rows, w_query, preferred_element_type=jnp.float32).astype(
        jnp.bfloat16
    )
    key_part = jnp.dot(piece_rows, w_key, preferred_element_type=jnp.float32).astype(jnp.bfloat16)
    value_part = jnp.dot(piece_rows, w_value, preferred_element_type=jnp.float32).astype(
        jnp.bfloat16
    )
    group_len = query_part.shape[0]
    block_count = group_len // BLOCK
    query_rows, key_rows, value_rows = (
        part.reshape(block_count, BLOCK, head_count, HEAD_DIM)
        for part in (query_part, key_part, value_part)
    )
    block_states = jnp.einsum(
        "bshd,bshe->bhde", key_rows, value_rows, preferred_element_type=jnp.float32
    )
    local_state = jnp.sum(block_states, axis=0)
    prefix_state = exclusive_scan(local_state, "ctx")
    running = jnp.cumsum(block_states, axis=0)
    earlier = jnp.concatenate([jnp.zeros_like(block_states), running[:-1]], axis=0)
    block_start = (prefix_state.astype(jnp.float32)[None] + earlier).astype(jnp.bfloat16)
    scores = jnp.einsum("bqhd,bkhd->bhqk", query_rows, key_rows, preferred_element_type=jnp.float32)
    causal = lax.broadcasted_iota(jnp.int32, scores.shape, 2) >= lax.broadcasted_iota(
        jnp.int32, scores.shape, 3
    )
    scores = jnp.where(causal, scores, jnp.float32(0.0)).astype(jnp.bfloat16)
    inner = jnp.einsum("bhqk,bkhe->bqhe", scores, value_rows, preferred_element_type=jnp.float32)
    inner = lax.optimization_barrier(inner)
    out = finish(
        query_rows.reshape(group_len, local_width),
        block_start.reshape(block_count * head_count, HEAD_DIM, HEAD_DIM),
        inner.reshape(group_len, local_width),
        norm_gain.reshape(1, local_width),
        head_count,
    )
    return out


def finish_kernel(query_ref, start_ref, inner_ref, gain_ref, out_ref):
    for head in range(start_ref.shape[0]):
        lanes = slice(head * HEAD_DIM, (head + 1) * HEAD_DIM)
        carried = jnp.dot(
            query_ref[:, lanes], start_ref[head], preferred_element_type=jnp.float32
        )
        mixed = inner_ref[:, lanes] + carried
        mean_square = jnp.mean(mixed * mixed, axis=-1, keepdims=True)
        normed = mixed * lax.rsqrt(mean_square + EPSILON) * gain_ref[:, lanes]
        out_ref[:, lanes] = normed.astype(out_ref.dtype)


def finish(query, start, inner, gain, head_count):
    rows, width = query.shape
    blocks = rows // BLOCK
    parts = 2
    tile = pl.BlockSpec((BLOCK // parts, width), lambda b, p: (b * parts + p, 0))
    return pl.pallas_call(
        finish_kernel,
        out_shape=jax.ShapeDtypeStruct(query.shape, jnp.bfloat16),
        grid=(blocks, parts),
        in_specs=[
            tile,
            pl.BlockSpec((head_count, HEAD_DIM, HEAD_DIM), lambda b, p: (b, 0, 0)),
            tile,
            pl.BlockSpec((1, width), lambda b, p: (0, 0)),
        ],
        out_specs=tile,
    )(query, start, inner, gain)


def chip_split(mesh):
    first = mesh.devices[0]
    cores = len({getattr(device, "core_on_chip", 0) for device in first})
    return mesh.devices.reshape(mesh.devices.shape[0], -1, cores)


def solution(mesh):
    fine = Mesh(chip_split(mesh), ("ctx", "y", "core"))
    heads = ("y", "core")
    placed = (P(("ctx",) + heads, None), P(None, heads), P(None, heads), P(None, heads), P(heads))
    return jax.shard_map(
        body, mesh=fine, in_specs=placed, out_specs=P("ctx", heads), check_vma=False
    )
```

```python
import jax
import jax.numpy as jnp
from jax import lax
from jax.experimental import pallas as pl
from jax.sharding import Mesh, PartitionSpec as P

HEAD_DIM = 128
BLOCK = 512


EPSILON = 1e-06


def from_behind(value, axis, by):
    size = lax.axis_size(axis)
    pairs = [(i, i + by) for i in range(size) if 0 <= i + by < size]
    return lax.ppermute(value, axis, pairs)


def exclusive_scan(value, axis):
    size = lax.axis_size(axis)
    pieces = value.reshape(size, -1, value.shape[-1]).astype(jnp.bfloat16)
    gathered = lax.all_to_all(pieces, axis, 0, 0, tiled=True)
    earlier = jnp.arange(size)[:, None] > jnp.arange(size)[None, :]
    before = jnp.dot(
        earlier.astype(gathered.dtype),
        gathered.reshape(size, -1),
        preferred_element_type=jnp.float32,
    ).astype(jnp.bfloat16)
    returned = lax.all_to_all(before.reshape(pieces.shape), axis, 0, 0, tiled=True)
    return returned.reshape(value.shape)


def spread(value, axis):
    size = lax.axis_size(axis)
    copies = jnp.broadcast_to(value[None], (size,) + value.shape)
    return lax.all_to_all(copies, axis, 0, 0, tiled=True)


def gather_rows(tokens):
    near = spread(tokens, "y")
    both = spread(near, "core")
    return both.transpose(1, 0, 2, 3).reshape(-1, tokens.shape[1])


def body(tokens, w_query, w_key, w_value, norm_gain):
    local_width = w_query.shape[1]
    head_count = local_width // HEAD_DIM
    piece_rows = gather_rows(tokens)
    query_part = jnp.dot(piece_rows, w_query, preferred_element_type=jnp.float32).astype(
        jnp.bfloat16
    )
    key_part = jnp.dot(piece_rows, w_key, preferred_element_type=jnp.float32).astype(jnp.bfloat16)
    value_part = jnp.dot(piece_rows, w_value, preferred_element_type=jnp.float32).astype(
        jnp.bfloat16
    )
    group_len = query_part.shape[0]
    block_count = group_len // BLOCK
    query_rows, key_rows, value_rows = (
        part.reshape(block_count, BLOCK, head_count, HEAD_DIM)
        for part in (query_part, key_part, value_part)
    )
    block_states = jnp.einsum(
        "bshd,bshe->bhde", key_rows, value_rows, preferred_element_type=jnp.float32
    )
    local_state = jnp.sum(block_states, axis=0)
    prefix_state = exclusive_scan(local_state, "ctx")
    running = jnp.cumsum(block_states, axis=0)
    earlier = jnp.concatenate([jnp.zeros_like(block_states), running[:-1]], axis=0)
    block_start = (prefix_state.astype(jnp.float32)[None] + earlier).astype(jnp.bfloat16)
    scores = jnp.einsum("bqhd,bkhd->bhqk", query_rows, key_rows, preferred_element_type=jnp.float32)
    causal = lax.broadcasted_iota(jnp.int32, scores.shape, 2) >= lax.broadcasted_iota(
        jnp.int32, scores.shape, 3
    )
    scores = jnp.where(causal, scores, jnp.float32(0.0)).astype(jnp.bfloat16)
    inner = jnp.einsum("bhqk,bkhe->bqhe", scores, value_rows, preferred_element_type=jnp.float32)
    inner = lax.optimization_barrier(inner)
    out = finish(
        query_rows.reshape(group_len, local_width),
        block_start.reshape(block_count * head_count, HEAD_DIM, HEAD_DIM),
        inner.reshape(group_len, local_width),
        norm_gain.reshape(1, local_width),
        head_count,
    )
    return out


def finish_kernel(query_ref, start_ref, inner_ref, gain_ref, out_ref):
    for head in range(start_ref.shape[0]):
        lanes = slice(head * HEAD_DIM, (head + 1) * HEAD_DIM)
        carried = jnp.dot(
            query_ref[:, lanes], start_ref[head], preferred_element_type=jnp.float32
        )
        mixed = inner_ref[:, lanes] + carried
        mean_square = jnp.mean(mixed * mixed, axis=-1, keepdims=True)
        normed = mixed * lax.rsqrt(mean_square + EPSILON) * gain_ref[:, lanes]
        out_ref[:, lanes] = normed.astype(out_ref.dtype)


def finish(query, start, inner, gain, head_count):
    rows, width = query.shape
    blocks = rows // BLOCK
    parts = 4
    tile = pl.BlockSpec((BLOCK // parts, width), lambda b, p: (b * parts + p, 0))
    return pl.pallas_call(
        finish_kernel,
        out_shape=jax.ShapeDtypeStruct(query.shape, jnp.bfloat16),
        grid=(blocks, parts),
        in_specs=[
            tile,
            pl.BlockSpec((head_count, HEAD_DIM, HEAD_DIM), lambda b, p: (b, 0, 0)),
            tile,
            pl.BlockSpec((1, width), lambda b, p: (0, 0)),
        ],
        out_specs=tile,
    )(query, start, inner, gain)


def chip_split(mesh):
    first = mesh.devices[0]
    cores = len({getattr(device, "core_on_chip", 0) for device in first})
    return mesh.devices.reshape(mesh.devices.shape[0], -1, cores)


def solution(mesh):
    fine = Mesh(chip_split(mesh), ("ctx", "y", "core"))
    heads = ("y", "core")
    placed = (P(("ctx",) + heads, None), P(None, heads), P(None, heads), P(None, heads), P(heads))
    return jax.shard_map(
        body, mesh=fine, in_specs=placed, out_specs=P("ctx", heads), check_vma=False
    )
```
